32 devices in a mesh: parts: 2 (over y), row: 4 (over x, core), col: 4 (over z).
Axes of the slice: x: 2, y: 2, z: 4, core: 2. Of those that a mesh axis runs over, the one named last changes fastest.
Arguments:
- basis: float32 [2048, 16384], P(('parts', 'row'), 'col'), parts along dimension 0, may hold values from -6 to 6
- panel_one: float32 [32768, 256], P(('parts', 'col', 'row')), parts along dimension 0, may hold values from -192 to 192
- panel_two: float32 [32768, 256], P(('parts', 'col', 'row')), parts along dimension 0, may hold values from -192 to 192
- gradient: float32 [2048, 512], P(('parts', 'row')), parts along dimension 0, may hold values from -0.25 to 0.25
Outputs:
- new_basis: float32 [2048, 16384], P(('parts', 'row'), 'col'), parts along dimension 0
- rotated: float32 [1024, 16384], P(('parts', 'row'), 'col'), parts along dimension 0
The draws below stay inside these ranges and needn't reach their ends.
There are 2 independent parts, one for each index of `parts`. The reference program is written for one: setup_inputs(seed, part) draws one part's arguments, and reference() takes and returns one part's arrays. A program takes and returns all parts, laid end to end along the dimension named above; each array names one. Nothing has to cross between parts.
All inputs are finite; a program needn't handle non-finite values.
Results may differ from the reference program's by a relative error of at most 0.0001.
Values sent between devices are 32-bit elements; how exact they have to be, the bound alone decides.
No kernel may reach another device: no remote copies, remote signals or barrier semaphores. Data moves between devices by JAX's collectives and lax.ppermute only.
A program may use at most 64 MiB of HBM per device.

```python
import math
import jax
import jax.numpy as jnp
from jax import lax

N = 16384
K = 256
GC = 512
ROWS = 1024


def make_panel(key, salt):
    key = jax.random.fold_in(key, salt)
    keys = jax.random.split(key, 4)
    noise = jnp.clip(jax.random.normal(keys[0], (N, K), jnp.float32), -4.0, 4.0)
    row_scale = jnp.exp(jax.random.uniform(keys[2], (N, 1), jnp.float32, 0.0, math.log(10.0)))
    shared = jnp.clip(jax.random.normal(keys[1], (N, 1), jnp.float32), -4.0, 4.0)
    col_scale = jnp.exp(jax.random.uniform(keys[3], (1, K), jnp.float32, 0.0, math.log(4.0)))
    return ((noise + 0.2 * shared) * row_scale * col_scale).astype(jnp.float32)


def draw_panel_one(key, part):
    return make_panel(key, 11)


def draw_panel_two(key, part):
    return make_panel(key, 23)


def spiked(array, stream_key, source, target, blocks, factor):
    owner, partner = [(jnp.arange(array.shape[position]) // (array.shape[position] // blocks)).reshape([-1 if axis == position else 1 for axis in range(array.ndim)]) for position in (source, target)]
    chosen = jax.random.permutation(stream_key, blocks)[partner]
    strong = (owner == chosen) | (owner == (partner + blocks // 2) % blocks)
    return jnp.where(strong, factor * array, array)


def levels(own_key, extent, cuts, low, largest):
    def one(axis_at, shards_of):
        heights = jax.random.uniform(jax.random.fold_in(jax.random.fold_in(own_key, 6), axis_at), (shards_of,), jnp.float32, low / len(cuts), largest / len(cuts))
        return jnp.repeat(jnp.exp(heights), extent[axis_at] // shards_of).reshape((-1,) + (1,) * (len(extent) - axis_at - 1))

    gain = one(*cuts[0])
    for cut in cuts[1:]:
        gain = gain * one(*cut)
    return gain


def normal_values(own_key, extent, scale, limit, cuts=(), kind=jnp.bfloat16):
    level = levels(own_key, extent, cuts, -0.22, 0.18) if cuts else 1.0
    drawn = jax.random.normal(own_key, extent, jnp.float32) * scale * level
    return jnp.minimum(jnp.maximum(drawn, -limit), limit).astype(kind)


def gaussian_with(key, shape, scale, reach, cuts, heavy, kind=jnp.bfloat16):
    entries = scale * jax.random.normal(key, shape, jnp.float32)
    if cuts:
        entries = entries * levels(key, shape, cuts, -0.22, 0.18)
    return jnp.clip(spiked(entries, jax.random.fold_in(key, 3), *heavy), -reach, reach).astype(kind)


def setup_inputs(seed: int = 0, part: int = 0) -> dict:
    splits = jax.random.split(jax.random.key(seed), 5)
    part_splits = jax.random.split(jax.random.fold_in(splits[4], part), 5)
    basis = normal_values(part_splits[0], (ROWS, N), 1.0, 6.0, ((0, 4), (1, 4)), jnp.float32)
    panel_one = draw_panel_one(jax.random.fold_in(jax.random.fold_in(splits[4], part), 71), part)
    panel_two = draw_panel_two(jax.random.fold_in(jax.random.fold_in(splits[4], part), 71), part)
    gradient = gaussian_with(part_splits[3], (ROWS, GC), ROWS ** -0.5, 0.25, ((0, 4),), (0, 1, 4, 2.0), jnp.float32)
    return dict(basis=basis, panel_one=panel_one, panel_two=panel_two, gradient=gradient)


def dot_high(left, right):
    return jnp.dot(left, right, precision=lax.Precision.HIGHEST, preferred_element_type=jnp.float32)


def tri_inverse(upper):
    size = upper.shape[0]
    width = 8
    count = size // width
    shaped = upper.reshape(count, width, count, width)
    selector = jnp.eye(count, dtype=upper.dtype)
    blocks = jnp.einsum("iajb,ij->iab", shaped, selector, precision=lax.Precision.HIGHEST)
    inverse = jnp.zeros_like(blocks)
    unit = jnp.eye(width, dtype=upper.dtype)
    for line in range(width - 1, -1, -1):
        known = jnp.einsum("bj,bjc->bc", blocks[:, line, :], inverse, precision=lax.Precision.HIGHEST)
        value = (unit[line][None, :] - known) / blocks[:, line, line][:, None]
        inverse = inverse.at[:, line, :].set(value)
    span = width
    while count > 1:
        shaped = upper.reshape(count, span, count, span)
        pairs = count // 2
        lefts = jnp.arange(pairs) * 2
        pick = ((jnp.arange(count)[None, :, None] == lefts[:, None, None]) & (jnp.arange(count)[None, None, :] == lefts[:, None, None] + 1)).astype(upper.dtype)
        corner = jnp.einsum("iajb,pij->pab", shaped, pick, precision=lax.Precision.HIGHEST)
        first = inverse[0::2]
        second = inverse[1::2]
        top = -jnp.einsum("pab,pbc->pac", jnp.einsum("pab,pbc->pac", first, corner, precision=lax.Precision.HIGHEST), second, precision=lax.Precision.HIGHEST)
        upper_half = jnp.concatenate([first, top], axis=2)
        lower_half = jnp.concatenate([jnp.zeros_like(second), second], axis=2)
        inverse = jnp.concatenate([upper_half, lower_half], axis=1)
        count = pairs
        span = span * 2
    return inverse[0]


def tri_factor(gram):
    upper = jnp.triu(gram, 1) + jnp.diag(jnp.diag(gram)) * 0.5
    return tri_inverse(upper)


def reference(basis, panel_one, panel_two, gradient):
    factor_one = tri_factor(dot_high(panel_one.T, panel_one))
    factor_two = tri_factor(dot_high(panel_two.T, panel_two))
    image_one = dot_high(basis, panel_one)
    middle = basis - dot_high(dot_high(image_one, factor_one), panel_one.T)
    image_two = dot_high(middle, panel_two)
    new_basis = middle - dot_high(dot_high(image_two, factor_two), panel_two.T)
    rotated = dot_high(gradient.T, new_basis)
    return new_basis, rotated
```

```python
import jax
import jax.numpy as jnp
from jax import lax
from jax.sharding import PartitionSpec as P


def dot_high(left, right):
    return jnp.dot(left, right, precision=lax.Precision.HIGHEST, preferred_element_type=jnp.float32)


def inner_rows(left, right):
    return jnp.einsum(
        "ra,rb->ab",
        left,
        right,
        precision=lax.Precision.HIGHEST,
        preferred_element_type=jnp.float32,
    )


def outer_cols(left, right):
    return jnp.einsum(
        "rk,ck->rc",
        left,
        right,
        precision=lax.Precision.HIGHEST,
        preferred_element_type=jnp.float32,
    )


def tri_inverse(upper):
    size = upper.shape[0]
    width = 8
    count = size // width
    shaped = upper.reshape(count, width, count, width)
    selector = jnp.eye(count, dtype=upper.dtype)
    blocks = jnp.einsum("iajb,ij->iab", shaped, selector, precision=lax.Precision.HIGHEST)
    inverse = jnp.zeros_like(blocks)
    unit = jnp.eye(width, dtype=upper.dtype)
    for line in range(width - 1, -1, -1):
        known = jnp.einsum(
            "bj,bjc->bc", blocks[:, line, :], inverse, precision=lax.Precision.HIGHEST
        )
        value = (unit[line][None, :] - known) / blocks[:, line, line][:, None]
        inverse = inverse.at[:, line, :].set(value)
    span = width
    while count > 1:
        shaped = upper.reshape(count, span, count, span)
        pairs = count // 2
        lefts = jnp.arange(pairs) * 2
        pick = (
            (jnp.arange(count)[None, :, None] == lefts[:, None, None])
            & (jnp.arange(count)[None, None, :] == lefts[:, None, None] + 1)
        ).astype(upper.dtype)
        corner = jnp.einsum("iajb,pij->pab", shaped, pick, precision=lax.Precision.HIGHEST)
        first = inverse[0::2]
        second = inverse[1::2]
        top = -jnp.einsum(
            "pab,pbc->pac",
            jnp.einsum("pab,pbc->pac", first, corner, precision=lax.Precision.HIGHEST),
            second,
            precision=lax.Precision.HIGHEST,
        )
        upper_half = jnp.concatenate([first, top], axis=2)
        lower_half = jnp.concatenate([jnp.zeros_like(second), second], axis=2)
        inverse = jnp.concatenate([upper_half, lower_half], axis=1)
        count = pairs
        span = span * 2
    return inverse[0]


def tri_factor(gram):
    upper = jnp.triu(gram, 1) + jnp.diag(jnp.diag(gram)) * 0.5
    return tri_inverse(upper)


def swap(value, distance, size):
    return lax.ppermute(value, "row", [(i, i ^ distance) for i in range(size)])


def spread(size):
    steps = []
    distance = 1
    while distance < size:
        steps.append(distance)
        distance *= 2
    return steps


def slot_order(me, size):
    steps = spread(size)
    order = []
    for slot in range(size):
        mask = 0
        for level, distance in enumerate(steps):
            if not (slot >> (len(steps) - 1 - level)) & 1:
                mask ^= distance
        order.append(mask)
    return jnp.array(order) ^ me


def scatter_rows(value, size):
    for distance in spread(size):
        count = value.shape[0] // 2
        value = value[count:] + swap(value[:count], distance, size)
    return value


def shards(basis, panel_one, panel_two, gradient):
    size = lax.axis_size("row")
    k = panel_one.shape[1]
    span = panel_one.shape[0]
    lanes = gradient.shape[1] // size
    me = lax.axis_index("row")
    own = jnp.concatenate([panel_one, panel_two], axis=1)
    held = {0: own}
    for distance in reversed(spread(size)):
        keys = sorted(held)
        got = swap(jnp.stack([held[key] for key in keys]), distance, size)
        for index, key in enumerate(keys):
            held[key ^ distance] = got[index]
    held = jnp.stack([held[key] for key in range(size)])

    gram_own = inner_rows(own, own)
    gram_chip = lax.psum(gram_own + swap(gram_own, 1, size), "col")
    half = me % 2
    rows = gram_chip.shape[0] // 2
    mine = lax.dynamic_slice_in_dim(gram_chip, half * rows, rows, axis=0)
    for distance in spread(size)[1:]:
        mine = mine + swap(mine, distance, size)
    halves = jnp.stack([mine, swap(mine, 1, size)])
    gram = jnp.take(halves, jnp.array([0, 1]) ^ half, axis=0).reshape(2 * rows, -1)

    order = slot_order(me, size)
    shuffled = jnp.take(gradient.reshape(-1, size, lanes), order, axis=1).reshape(gradient.shape)
    head = inner_rows(shuffled, basis)
    count = head.shape[0] // 2
    head = head[count:] + swap(head[:count], 1, size)
    head, _ = lax.optimization_barrier((head, held))
    for distance in spread(size)[1:]:
        count = head.shape[0] // 2
        head = head[count:] + swap(head[:count], distance, size)

    image = None
    for slot in range(size):
        cols = lax.dynamic_slice_in_dim(basis, (me ^ slot) * span, span, axis=1)
        part = dot_high(cols, held[slot])
        image = part if image is None else image + part
    image, gram = lax.optimization_barrier((image, gram))
    image = lax.psum(image, "col")

    gathered = jnp.take(held, jnp.arange(size) ^ me, axis=0).reshape(size * span, -1)
    factor_one = tri_factor(gram[:k, :k])
    factor_two = tri_factor(gram[k:, k:])
    first = dot_high(image[:, :k], factor_one)
    image_two = image[:, k:] - dot_high(first, gram[:k, k:])
    second = dot_high(image_two, factor_two)
    weight = jnp.concatenate([first, second], axis=1)
    new_basis = basis - outer_cols(weight, gathered)
    tail = scatter_rows(inner_rows(shuffled, weight), size)
    rotated = head - outer_cols(tail, gathered)
    return (new_basis, rotated)


def solution(mesh):
    return jax.shard_map(
        shards,
        mesh=mesh,
        in_specs=(
            P(("parts", "row"), "col"),
            P(("parts", "col", "row"), None),
            P(("parts", "col", "row"), None),
            P(("parts", "row"), None),
        ),
        out_specs=(P(("parts", "row"), "col"), P(("parts", "row"), "col")),
        check_vma=False,
    )
```

```python
import jax
import jax.numpy as jnp
from jax import lax
from jax.sharding import PartitionSpec as P


def dot_high(left, right):
    return jnp.dot(left, right, precision=lax.Precision.HIGHEST, preferred_element_type=jnp.float32)


def inner_rows(left, right):
    return jnp.einsum(
        "ra,rb->ab",
        left,
        right,
        precision=lax.Precision.HIGHEST,
        preferred_element_type=jnp.float32,
    )


def outer_cols(left, right):
    return jnp.einsum(
        "rk,ck->rc",
        left,
        right,
        precision=lax.Precision.HIGHEST,
        preferred_element_type=jnp.float32,
    )


def tri_inverse(upper):
    size = upper.shape[0]
    width = 8
    count = size // width
    shaped = upper.reshape(count, width, count, width)
    selector = jnp.eye(count, dtype=upper.dtype)
    blocks = jnp.einsum("iajb,ij->iab", shaped, selector, precision=lax.Precision.HIGHEST)
    inverse = jnp.zeros_like(blocks)
    unit = jnp.eye(width, dtype=upper.dtype)
    for line in range(width - 1, -1, -1):
        known = jnp.einsum(
            "bj,bjc->bc", blocks[:, line, :], inverse, precision=lax.Precision.HIGHEST
        )
        value = (unit[line][None, :] - known) / blocks[:, line, line][:, None]
        inverse = inverse.at[:, line, :].set(value)
    span = width
    while count > 1:
        shaped = upper.reshape(count, span, count, span)
        pairs = count // 2
        lefts = jnp.arange(pairs) * 2
        pick = (
            (jnp.arange(count)[None, :, None] == lefts[:, None, None])
            & (jnp.arange(count)[None, None, :] == lefts[:, None, None] + 1)
        ).astype(upper.dtype)
        corner = jnp.einsum("iajb,pij->pab", shaped, pick, precision=lax.Precision.HIGHEST)
        first = inverse[0::2]
        second = inverse[1::2]
        top = -jnp.einsum(
            "pab,pbc->pac",
            jnp.einsum("pab,pbc->pac", first, corner, precision=lax.Precision.HIGHEST),
            second,
            precision=lax.Precision.HIGHEST,
        )
        upper_half = jnp.concatenate([first, top], axis=2)
        lower_half = jnp.concatenate([jnp.zeros_like(second), second], axis=2)
        inverse = jnp.concatenate([upper_half, lower_half], axis=1)
        count = pairs
        span = span * 2
    return inverse[0]


def tri_factor(gram):
    upper = jnp.triu(gram, 1) + jnp.diag(jnp.diag(gram)) * 0.5
    return tri_inverse(upper)


def swap(value, distance, size):
    return lax.ppermute(value, "row", [(i, i ^ distance) for i in range(size)])


def spread(size):
    steps = []
    distance = 1
    while distance < size:
        steps.append(distance)
        distance *= 2
    return steps


def slot_order(me, size):
    steps = spread(size)
    order = []
    for slot in range(size):
        mask = 0
        for level, distance in enumerate(steps):
            if not (slot >> (len(steps) - 1 - level)) & 1:
                mask ^= distance
        order.append(mask)
    return jnp.array(order) ^ me


def col_sum(value):
    size = lax.axis_size("col")
    for distance in spread(size):
        value = value + lax.ppermute(
            value, "col", [(i, i ^ distance) for i in range(size)]
        )
    return value


def scatter_rows(value, size):
    for distance in spread(size):
        count = value.shape[0] // 2
        value = value[count:] + swap(value[:count], distance, size)
    return value


def shards(basis, panel_one, panel_two, gradient):
    size = lax.axis_size("row")
    k = panel_one.shape[1]
    span = panel_one.shape[0]
    lanes = gradient.shape[1] // size
    me = lax.axis_index("row")
    own = jnp.concatenate([panel_one, panel_two], axis=1)
    held = {0: own}
    for distance in reversed(spread(size)):
        keys = sorted(held)
        got = swap(jnp.stack([held[key] for key in keys]), distance, size)
        for index, key in enumerate(keys):
            held[key ^ distance] = got[index]
    held = jnp.stack([held[key] for key in range(size)])

    gram_own = inner_rows(own, own)
    gram_chip = gram_own + swap(gram_own, 1, size)
    half = me % 2
    rows = gram_chip.shape[0] // 2
    mine = col_sum(lax.dynamic_slice_in_dim(gram_chip, half * rows, rows, axis=0))
    for distance in spread(size)[1:]:
        mine = mine + swap(mine, distance, size)
    halves = jnp.stack([mine, swap(mine, 1, size)])
    gram = jnp.take(halves, jnp.array([0, 1]) ^ half, axis=0).reshape(2 * rows, -1)

    order = slot_order(me, size)
    shuffled = jnp.take(gradient.reshape(-1, size, lanes), order, axis=1).reshape(gradient.shape)
    head = inner_rows(shuffled, basis)
    count = head.shape[0] // 2
    head = head[count:] + swap(head[:count], 1, size)
    head, _ = lax.optimization_barrier((head, held))
    for distance in spread(size)[1:]:
        count = head.shape[0] // 2
        head = head[count:] + swap(head[:count], distance, size)

    image = None
    for slot in range(size):
        cols = lax.dynamic_slice_in_dim(basis, (me ^ slot) * span, span, axis=1)
        part = dot_high(cols, held[slot])
        image = part if image is None else image + part
    image = col_sum(image)

    gathered = jnp.take(held, jnp.arange(size) ^ me, axis=0).reshape(size * span, -1)
    factor_one = tri_factor(gram[:k, :k])
    factor_two = tri_factor(gram[k:, k:])
    first = dot_high(image[:, :k], factor_one)
    image_two = image[:, k:] - dot_high(first, gram[:k, k:])
    second = dot_high(image_two, factor_two)
    weight = jnp.concatenate([first, second], axis=1)
    new_basis = basis - outer_cols(weight, gathered)
    tail = scatter_rows(inner_rows(shuffled, weight), size)
    rotated = head - outer_cols(tail, gathered)
    return (new_basis, rotated)


def solution(mesh):
    return jax.shard_map(
        shards,
        mesh=mesh,
        in_specs=(
            P(("parts", "row"), "col"),
            P(("parts", "col", "row"), None),
            P(("parts", "col", "row"), None),
            P(("parts", "row"), None),
        ),
        out_specs=(P(("parts", "row"), "col"), P(("parts", "row"), "col")),
        check_vma=False,
    )
```

```python
import jax
import jax.numpy as jnp
from jax import lax
from jax.sharding import PartitionSpec as P


def dot_high(left, right):
    return jnp.dot(left, right, precision=lax.Precision.HIGHEST, preferred_element_type=jnp.float32)


def inner_rows(left, right):
    return jnp.einsum(
        "ra,rb->ab",
        left,
        right,
        precision=lax.Precision.HIGHEST,
        preferred_element_type=jnp.float32,
    )


def outer_cols(left, right):
    return jnp.einsum(
        "rk,ck->rc",
        left,
        right,
        precision=lax.Precision.HIGHEST,
        preferred_element_type=jnp.float32,
    )


def tri_inverse(upper):
    size = upper.shape[0]
    width = 8
    count = size // width
    shaped = upper.reshape(count, width, count, width)
    selector = jnp.eye(count, dtype=upper.dtype)
    blocks = jnp.einsum("iajb,ij->iab", shaped, selector, precision=lax.Precision.HIGHEST)
    inverse = jnp.zeros_like(blocks)
    unit = jnp.eye(width, dtype=upper.dtype)
    for line in range(width - 1, -1, -1):
        known = jnp.einsum(
            "bj,bjc->bc", blocks[:, line, :], inverse, precision=lax.Precision.HIGHEST
        )
        value = (unit[line][None, :] - known) / blocks[:, line, line][:, None]
        inverse = inverse.at[:, line, :].set(value)
    span = width
    while count > 1:
        shaped = upper.reshape(count, span, count, span)
        pairs = count // 2
        lefts = jnp.arange(pairs) * 2
        pick = (
            (jnp.arange(count)[None, :, None] == lefts[:, None, None])
            & (jnp.arange(count)[None, None, :] == lefts[:, None, None] + 1)
        ).astype(upper.dtype)
        corner = jnp.einsum("iajb,pij->pab", shaped, pick, precision=lax.Precision.HIGHEST)
        first = inverse[0::2]
        second = inverse[1::2]
        top = -jnp.einsum(
            "pab,pbc->pac",
            jnp.einsum("pab,pbc->pac", first, corner, precision=lax.Precision.HIGHEST),
            second,
            precision=lax.Precision.HIGHEST,
        )
        upper_half = jnp.concatenate([first, top], axis=2)
        lower_half = jnp.concatenate([jnp.zeros_like(second), second], axis=2)
        inverse = jnp.concatenate([upper_half, lower_half], axis=1)
        count = pairs
        span = span * 2
    return inverse[0]


def tri_factor(gram):
    upper = jnp.triu(gram, 1) + jnp.diag(jnp.diag(gram)) * 0.5
    return tri_inverse(upper)


def tri_inverse_pair(uppers):
    size = uppers[0].shape[0]
    width = 8
    count = size // width
    selector = jnp.eye(count, dtype=uppers[0].dtype)
    blocks = jnp.concatenate(
        [
            jnp.einsum(
                "iajb,ij->iab",
                upper.reshape(count, width, count, width),
                selector,
                precision=lax.Precision.HIGHEST,
            )
            for upper in uppers
        ],
        axis=0,
    )
    inverse = jnp.zeros_like(blocks)
    unit = jnp.eye(width, dtype=blocks.dtype)
    for line in range(width - 1, -1, -1):
        known = jnp.einsum(
            "bj,bjc->bc", blocks[:, line, :], inverse, precision=lax.Precision.HIGHEST
        )
        value = (unit[line][None, :] - known) / blocks[:, line, line][:, None]
        inverse = inverse.at[:, line, :].set(value)
    span = width
    while count > 1:
        pairs = count // 2
        lefts = jnp.arange(pairs) * 2
        pick = (
            (jnp.arange(count)[None, :, None] == lefts[:, None, None])
            & (jnp.arange(count)[None, None, :] == lefts[:, None, None] + 1)
        ).astype(blocks.dtype)
        corner = jnp.concatenate(
            [
                jnp.einsum(
                    "iajb,pij->pab",
                    upper.reshape(count, span, count, span),
                    pick,
                    precision=lax.Precision.HIGHEST,
                )
                for upper in uppers
            ],
            axis=0,
        )
        first = inverse[0::2]
        second = inverse[1::2]
        top = -jnp.einsum(
            "pab,pbc->pac",
            jnp.einsum("pab,pbc->pac", first, corner, precision=lax.Precision.HIGHEST),
            second,
            precision=lax.Precision.HIGHEST,
        )
        upper_half = jnp.concatenate([first, top], axis=2)
        lower_half = jnp.concatenate([jnp.zeros_like(second), second], axis=2)
        inverse = jnp.concatenate([upper_half, lower_half], axis=1)
        count = pairs
        span = span * 2
    return inverse[0], inverse[1]


def tri_factor_pair(grams):
    return tri_inverse_pair(
        [jnp.triu(gram, 1) + jnp.diag(jnp.diag(gram)) * 0.5 for gram in grams]
    )


def swap(value, distance, size):
    return lax.ppermute(value, "row", [(i, i ^ distance) for i in range(size)])


def spread(size):
    steps = []
    distance = 1
    while distance < size:
        steps.append(distance)
        distance *= 2
    return steps


def slot_order(me, size):
    steps = spread(size)
    order = []
    for slot in range(size):
        mask = 0
        for level, distance in enumerate(steps):
            if not (slot >> (len(steps) - 1 - level)) & 1:
                mask ^= distance
        order.append(mask)
    return jnp.array(order) ^ me


def col_sum(value):
    size = lax.axis_size("col")
    for distance in spread(size):
        value = value + lax.ppermute(
            value, "col", [(i, i ^ distance) for i in range(size)]
        )
    return value


def scatter_rows(value, size):
    for distance in spread(size):
        count = value.shape[0] // 2
        value = value[count:] + swap(value[:count], distance, size)
    return value


def shards(basis, panel_one, panel_two, gradient):
    size = lax.axis_size("row")
    k = panel_one.shape[1]
    span = panel_one.shape[0]
    lanes = gradient.shape[1] // size
    me = lax.axis_index("row")
    own = jnp.concatenate([panel_one, panel_two], axis=1)
    held = {0: own}
    for distance in reversed(spread(size)):
        keys = sorted(held)
        got = swap(jnp.stack([held[key] for key in keys]), distance, size)
        for index, key in enumerate(keys):
            held[key ^ distance] = got[index]
    held = jnp.stack([held[key] for key in range(size)])

    gram_own = inner_rows(own, own)
    gram_chip = gram_own + swap(gram_own, 1, size)
    half = me % 2
    rows = gram_chip.shape[0] // 2
    mine = col_sum(lax.dynamic_slice_in_dim(gram_chip, half * rows, rows, axis=0))
    for distance in spread(size)[1:]:
        mine = mine + swap(mine, distance, size)
    halves = jnp.stack([mine, swap(mine, 1, size)])
    gram = jnp.take(halves, jnp.array([0, 1]) ^ half, axis=0).reshape(2 * rows, -1)

    order = slot_order(me, size)
    shuffled = jnp.take(gradient.reshape(-1, size, lanes), order, axis=1).reshape(gradient.shape)
    head = inner_rows(shuffled, basis)
    count = head.shape[0] // 2
    head = head[count:] + swap(head[:count], 1, size)
    head, _ = lax.optimization_barrier((head, held))
    for distance in spread(size)[1:]:
        count = head.shape[0] // 2
        head = head[count:] + swap(head[:count], distance, size)

    image = None
    for slot in range(size):
        cols = lax.dynamic_slice_in_dim(basis, (me ^ slot) * span, span, axis=1)
        part = dot_high(cols, held[slot])
        image = part if image is None else image + part
    image = col_sum(image)

    gathered = jnp.take(held, jnp.arange(size) ^ me, axis=0).reshape(size * span, -1)
    factor_one, factor_two = tri_factor_pair([gram[:k, :k], gram[k:, k:]])
    first = dot_high(image[:, :k], factor_one)
    image_two = image[:, k:] - dot_high(first, gram[:k, k:])
    second = dot_high(image_two, factor_two)
    weight = jnp.concatenate([first, second], axis=1)
    new_basis = basis - outer_cols(weight, gathered)
    tail = scatter_rows(inner_rows(shuffled, weight), size)
    rotated = head - outer_cols(tail, gathered)
    return (new_basis, rotated)


def solution(mesh):
    return jax.shard_map(
        shards,
        mesh=mesh,
        in_specs=(
            P(("parts", "row"), "col"),
            P(("parts", "col", "row"), None),
            P(("parts", "col", "row"), None),
            P(("parts", "row"), None),
        ),
        out_specs=(P(("parts", "row"), "col"), P(("parts", "row"), "col")),
        check_vma=False,
    )
```

```python
import jax
import jax.numpy as jnp
from jax import lax
from jax.sharding import PartitionSpec as P


def dot_high(left, right):
    return jnp.dot(left, right, precision=lax.Precision.HIGHEST, preferred_element_type=jnp.float32)


def inner_rows(left, right):
    return jnp.einsum(
        "ra,rb->ab",
        left,
        right,
        precision=lax.Precision.HIGHEST,
        preferred_element_type=jnp.float32,
    )


def outer_cols(left, right):
    return jnp.einsum(
        "rk,ck->rc",
        left,
        right,
        precision=lax.Precision.HIGHEST,
        preferred_element_type=jnp.float32,
    )


def tri_inverse(upper):
    size = upper.shape[0]
    width = 8
    count = size // width
    shaped = upper.reshape(count, width, count, width)
    selector = jnp.eye(count, dtype=upper.dtype)
    blocks = jnp.einsum("iajb,ij->iab", shaped, selector, precision=lax.Precision.HIGHEST)
    inverse = jnp.zeros_like(blocks)
    unit = jnp.eye(width, dtype=upper.dtype)
    for line in range(width - 1, -1, -1):
        known = jnp.einsum(
            "bj,bjc->bc", blocks[:, line, :], inverse, precision=lax.Precision.HIGHEST
        )
        value = (unit[line][None, :] - known) / blocks[:, line, line][:, None]
        inverse = inverse.at[:, line, :].set(value)
    span = width
    while count > 1:
        shaped = upper.reshape(count, span, count, span)
        pairs = count // 2
        lefts = jnp.arange(pairs) * 2
        pick = (
            (jnp.arange(count)[None, :, None] == lefts[:, None, None])
            & (jnp.arange(count)[None, None, :] == lefts[:, None, None] + 1)
        ).astype(upper.dtype)
        corner = jnp.einsum("iajb,pij->pab", shaped, pick, precision=lax.Precision.HIGHEST)
        first = inverse[0::2]
        second = inverse[1::2]
        top = -jnp.einsum(
            "pab,pbc->pac",
            jnp.einsum("pab,pbc->pac", first, corner, precision=lax.Precision.HIGHEST),
            second,
            precision=lax.Precision.HIGHEST,
        )
        upper_half = jnp.concatenate([first, top], axis=2)
        lower_half = jnp.concatenate([jnp.zeros_like(second), second], axis=2)
        inverse = jnp.concatenate([upper_half, lower_half], axis=1)
        count = pairs
        span = span * 2
    return inverse[0]


def tri_factor(gram):
    upper = jnp.triu(gram, 1) + jnp.diag(jnp.diag(gram)) * 0.5
    return tri_inverse(upper)


def tri_factor_doubling(gram):
    size = gram.shape[0]
    upper = jnp.triu(gram, 1) + jnp.diag(jnp.diag(gram)) * 0.5
    index = jnp.arange(size)
    same = index[:, None] == index[None, :]
    inverse = jnp.where(same, 1.0 / jnp.diag(upper)[None, :], 0.0)
    span = 1
    while span < size:
        group = index // (2 * span)
        side = (index // span) % 2
        corner = (group[:, None] == group[None, :]) & (side[:, None] == 0) & (side[None, :] == 1)
        inverse = inverse - dot_high(dot_high(inverse, jnp.where(corner, upper, 0.0)), inverse)
        span *= 2
    return inverse


def swap(value, distance, size):
    return lax.ppermute(value, "row", [(i, i ^ distance) for i in range(size)])


def spread(size):
    steps = []
    distance = 1
    while distance < size:
        steps.append(distance)
        distance *= 2
    return steps


def slot_order(me, size):
    steps = spread(size)
    order = []
    for slot in range(size):
        mask = 0
        for level, distance in enumerate(steps):
            if not (slot >> (len(steps) - 1 - level)) & 1:
                mask ^= distance
        order.append(mask)
    return jnp.array(order) ^ me


def col_sum(value):
    size = lax.axis_size("col")
    for distance in spread(size):
        value = value + lax.ppermute(
            value, "col", [(i, i ^ distance) for i in range(size)]
        )
    return value


def scatter_rows(value, size):
    for distance in spread(size):
        count = value.shape[0] // 2
        value = value[count:] + swap(value[:count], distance, size)
    return value


def shards(basis, panel_one, panel_two, gradient):
    size = lax.axis_size("row")
    k = panel_one.shape[1]
    span = panel_one.shape[0]
    lanes = gradient.shape[1] // size
    me = lax.axis_index("row")
    own = jnp.concatenate([panel_one, panel_two], axis=1)
    held = {0: own}
    for distance in reversed(spread(size)):
        keys = sorted(held)
        got = swap(jnp.stack([held[key] for key in keys]), distance, size)
        for index, key in enumerate(keys):
            held[key ^ distance] = got[index]
    held = jnp.stack([held[key] for key in range(size)])

    gram_own = inner_rows(own, own)
    gram_chip = gram_own + swap(gram_own, 1, size)
    half = me % 2
    rows = gram_chip.shape[0] // 2
    mine = col_sum(lax.dynamic_slice_in_dim(gram_chip, half * rows, rows, axis=0))
    for distance in spread(size)[1:]:
        mine = mine + swap(mine, distance, size)
    halves = jnp.stack([mine, swap(mine, 1, size)])
    gram = jnp.take(halves, jnp.array([0, 1]) ^ half, axis=0).reshape(2 * rows, -1)

    order = slot_order(me, size)
    shuffled = jnp.take(gradient.reshape(-1, size, lanes), order, axis=1).reshape(gradient.shape)
    head = inner_rows(shuffled, basis)
    count = head.shape[0] // 2
    head = head[count:] + swap(head[:count], 1, size)
    head, _ = lax.optimization_barrier((head, held))
    for distance in spread(size)[1:]:
        count = head.shape[0] // 2
        head = head[count:] + swap(head[:count], distance, size)

    image = None
    for slot in range(size):
        cols = lax.dynamic_slice_in_dim(basis, (me ^ slot) * span, span, axis=1)
        part = dot_high(cols, held[slot])
        image = part if image is None else image + part
    image = col_sum(image)

    gathered = jnp.take(held, jnp.arange(size) ^ me, axis=0).reshape(size * span, -1)
    factor_one = tri_factor_doubling(gram[:k, :k])
    factor_two = tri_factor_doubling(gram[k:, k:])
    first = dot_high(image[:, :k], factor_one)
    image_two = image[:, k:] - dot_high(first, gram[:k, k:])
    second = dot_high(image_two, factor_two)
    weight = jnp.concatenate([first, second], axis=1)
    new_basis = basis - outer_cols(weight, gathered)
    tail = scatter_rows(inner_rows(shuffled, weight), size)
    rotated = head - outer_cols(tail, gathered)
    return (new_basis, rotated)


def solution(mesh):
    return jax.shard_map(
        shards,
        mesh=mesh,
        in_specs=(
            P(("parts", "row"), "col"),
            P(("parts", "col", "row"), None),
            P(("parts", "col", "row"), None),
            P(("parts", "row"), None),
        ),
        out_specs=(P(("parts", "row"), "col"), P(("parts", "row"), "col")),
        check_vma=False,
    )
```

```python
import jax
import jax.numpy as jnp
from jax import lax
from jax.sharding import PartitionSpec as P


def dot_high(left, right):
    return jnp.dot(left, right, precision=lax.Precision.HIGHEST, preferred_element_type=jnp.float32)


def inner_rows(left, right):
    return jnp.einsum(
        "ra,rb->ab",
        left,
        right,
        precision=lax.Precision.HIGHEST,
        preferred_element_type=jnp.float32,
    )


def outer_cols(left, right):
    return jnp.einsum(
        "rk,ck->rc",
        left,
        right,
        precision=lax.Precision.HIGHEST,
        preferred_element_type=jnp.float32,
    )


def tri_inverse(upper):
    size = upper.shape[0]
    width = 8
    count = size // width
    shaped = upper.reshape(count, width, count, width)
    selector = jnp.eye(count, dtype=upper.dtype)
    blocks = jnp.einsum("iajb,ij->iab", shaped, selector, precision=lax.Precision.HIGHEST)
    inverse = jnp.zeros_like(blocks)
    unit = jnp.eye(width, dtype=upper.dtype)
    for line in range(width - 1, -1, -1):
        known = jnp.einsum(
            "bj,bjc->bc", blocks[:, line, :], inverse, precision=lax.Precision.HIGHEST
        )
        value = (unit[line][None, :] - known) / blocks[:, line, line][:, None]
        inverse = inverse.at[:, line, :].set(value)
    span = width
    while count > 1:
        shaped = upper.reshape(count, span, count, span)
        pairs = count // 2
        lefts = jnp.arange(pairs) * 2
        pick = (
            (jnp.arange(count)[None, :, None] == lefts[:, None, None])
            & (jnp.arange(count)[None, None, :] == lefts[:, None, None] + 1)
        ).astype(upper.dtype)
        corner = jnp.einsum("iajb,pij->pab", shaped, pick, precision=lax.Precision.HIGHEST)
        first = inverse[0::2]
        second = inverse[1::2]
        top = -jnp.einsum(
            "pab,pbc->pac",
            jnp.einsum("pab,pbc->pac", first, corner, precision=lax.Precision.HIGHEST),
            second,
            precision=lax.Precision.HIGHEST,
        )
        upper_half = jnp.concatenate([first, top], axis=2)
        lower_half = jnp.concatenate([jnp.zeros_like(second), second], axis=2)
        inverse = jnp.concatenate([upper_half, lower_half], axis=1)
        count = pairs
        span = span * 2
    return inverse[0]


def tri_factor(gram):
    upper = jnp.triu(gram, 1) + jnp.diag(jnp.diag(gram)) * 0.5
    return tri_inverse(upper)


def tri_factor_doubling(gram):
    size = gram.shape[0]
    upper = jnp.triu(gram, 1) + jnp.diag(jnp.diag(gram)) * 0.5
    index = jnp.arange(size)
    same = index[:, None] == index[None, :]
    inverse = jnp.where(same, 1.0 / jnp.diag(upper)[None, :], 0.0)
    span = 1
    while span < size:
        group = index // (2 * span)
        side = (index // span) % 2
        corner = (group[:, None] == group[None, :]) & (side[:, None] == 0) & (side[None, :] == 1)
        inverse = inverse - dot_high(dot_high(inverse, jnp.where(corner, upper, 0.0)), inverse)
        span *= 2
    return inverse


def swap(value, distance, size):
    return lax.ppermute(value, "row", [(i, i ^ distance) for i in range(size)])


def spread(size):
    steps = []
    distance = 1
    while distance < size:
        steps.append(distance)
        distance *= 2
    return steps


def slot_order(me, size):
    steps = spread(size)
    order = []
    for slot in range(size):
        mask = 0
        for level, distance in enumerate(steps):
            if not (slot >> (len(steps) - 1 - level)) & 1:
                mask ^= distance
        order.append(mask)
    return jnp.array(order) ^ me


def col_sum(value):
    size = lax.axis_size("col")
    for distance in spread(size):
        value = value + lax.ppermute(
            value, "col", [(i, i ^ distance) for i in range(size)]
        )
    return value


def scatter_rows(value, size):
    for distance in spread(size):
        count = value.shape[0] // 2
        value = value[count:] + swap(value[:count], distance, size)
    return value


def shards(basis, panel_one, panel_two, gradient):
    size = lax.axis_size("row")
    k = panel_one.shape[1]
    span = panel_one.shape[0]
    lanes = gradient.shape[1] // size
    me = lax.axis_index("row")
    own = jnp.concatenate([panel_one, panel_two], axis=1)
    held = {0: own}
    beside = swap(own, 1, size)
    for distance in reversed(spread(size)):
        keys = [key for key in sorted(held) if distance > 1 or key]
        if distance == 1:
            held[1] = beside
        if keys:
            got = swap(jnp.stack([held[key] for key in keys]), distance, size)
            for index, key in enumerate(keys):
                held[key ^ distance] = got[index]
    held = jnp.stack([held[key] for key in range(size)])

    gram_own = inner_rows(own, own)
    gram_chip = gram_own + swap(gram_own, 1, size)
    half = me % 2
    rows = gram_chip.shape[0] // 2
    mine = col_sum(lax.dynamic_slice_in_dim(gram_chip, half * rows, rows, axis=0))
    for distance in spread(size)[1:]:
        mine = mine + swap(mine, distance, size)
    halves = jnp.stack([mine, swap(mine, 1, size)])
    gram = jnp.take(halves, jnp.array([0, 1]) ^ half, axis=0).reshape(2 * rows, -1)

    order = slot_order(me, size)
    shuffled = jnp.take(gradient.reshape(-1, size, lanes), order, axis=1).reshape(gradient.shape)
    head = inner_rows(shuffled, basis)
    count = head.shape[0] // 2
    head = head[count:] + swap(head[:count], 1, size)
    head, _ = lax.optimization_barrier((head, held))
    for distance in spread(size)[1:]:
        count = head.shape[0] // 2
        head = head[count:] + swap(head[:count], distance, size)

    image = None
    for slot in range(size):
        cols = lax.dynamic_slice_in_dim(basis, (me ^ slot) * span, span, axis=1)
        part = dot_high(cols, held[slot])
        image = part if image is None else image + part
    image = col_sum(image)

    gathered = jnp.take(held, jnp.arange(size) ^ me, axis=0).reshape(size * span, -1)
    factor_one = tri_factor_doubling(gram[:k, :k])
    factor_two = tri_factor_doubling(gram[k:, k:])
    first = dot_high(image[:, :k], factor_one)
    image_two = image[:, k:] - dot_high(first, gram[:k, k:])
    second = dot_high(image_two, factor_two)
    weight = jnp.concatenate([first, second], axis=1)
    new_basis = basis - outer_cols(weight, gathered)
    tail = scatter_rows(inner_rows(shuffled, weight), size)
    rotated = head - outer_cols(tail, gathered)
    return (new_basis, rotated)


def solution(mesh):
    return jax.shard_map(
        shards,
        mesh=mesh,
        in_specs=(
            P(("parts", "row"), "col"),
            P(("parts", "col", "row"), None),
            P(("parts", "col", "row"), None),
            P(("parts", "row"), None),
        ),
        out_specs=(P(("parts", "row"), "col"), P(("parts", "row"), "col")),
        check_vma=False,
    )
```

```python
import jax
import jax.numpy as jnp
from jax import lax
from jax.sharding import PartitionSpec as P


def dot_high(left, right):
    return jnp.dot(left, right, precision=lax.Precision.HIGHEST, preferred_element_type=jnp.float32)


def inner_rows(left, right):
    return jnp.einsum(
        "ra,rb->ab",
        left,
        right,
        precision=lax.Precision.HIGHEST,
        preferred_element_type=jnp.float32,
    )


def outer_cols(left, right):
    return jnp.einsum(
        "rk,ck->rc",
        left,
        right,
        precision=lax.Precision.HIGHEST,
        preferred_element_type=jnp.float32,
    )


def tri_inverse(upper):
    size = upper.shape[0]
    width = 8
    count = size // width
    shaped = upper.reshape(count, width, count, width)
    selector = jnp.eye(count, dtype=upper.dtype)
    blocks = jnp.einsum("iajb,ij->iab", shaped, selector, precision=lax.Precision.HIGHEST)
    inverse = jnp.zeros_like(blocks)
    unit = jnp.eye(width, dtype=upper.dtype)
    for line in range(width - 1, -1, -1):
        known = jnp.einsum(
            "bj,bjc->bc", blocks[:, line, :], inverse, precision=lax.Precision.HIGHEST
        )
        value = (unit[line][None, :] - known) / blocks[:, line, line][:, None]
        inverse = inverse.at[:, line, :].set(value)
    span = width
    while count > 1:
        shaped = upper.reshape(count, span, count, span)
        pairs = count // 2
        lefts = jnp.arange(pairs) * 2
        pick = (
            (jnp.arange(count)[None, :, None] == lefts[:, None, None])
            & (jnp.arange(count)[None, None, :] == lefts[:, None, None] + 1)
        ).astype(upper.dtype)
        corner = jnp.einsum("iajb,pij->pab", shaped, pick, precision=lax.Precision.HIGHEST)
        first = inverse[0::2]
        second = inverse[1::2]
        top = -jnp.einsum(
            "pab,pbc->pac",
            jnp.einsum("pab,pbc->pac", first, corner, precision=lax.Precision.HIGHEST),
            second,
            precision=lax.Precision.HIGHEST,
        )
        upper_half = jnp.concatenate([first, top], axis=2)
        lower_half = jnp.concatenate([jnp.zeros_like(second), second], axis=2)
        inverse = jnp.concatenate([upper_half, lower_half], axis=1)
        count = pairs
        span = span * 2
    return inverse[0]


def tri_factor(gram):
    upper = jnp.triu(gram, 1) + jnp.diag(jnp.diag(gram)) * 0.5
    return tri_inverse(upper)


def tri_factor_doubling(gram):
    size = gram.shape[0]
    upper = jnp.triu(gram, 1) + jnp.diag(jnp.diag(gram)) * 0.5
    index = jnp.arange(size)
    same = index[:, None] == index[None, :]
    inverse = jnp.where(same, 1.0 / jnp.diag(upper)[None, :], 0.0)
    span = 1
    while span < size:
        group = index // (2 * span)
        side = (index // span) % 2
        corner = (group[:, None] == group[None, :]) & (side[:, None] == 0) & (side[None, :] == 1)
        inverse = inverse - dot_high(dot_high(inverse, jnp.where(corner, upper, 0.0)), inverse)
        span *= 2
    return inverse


def swap(value, distance, size):
    return lax.ppermute(value, "row", [(i, i ^ distance) for i in range(size)])


def spread(size):
    steps = []
    distance = 1
    while distance < size:
        steps.append(distance)
        distance *= 2
    return steps


def slot_order(me, size):
    steps = spread(size)
    order = []
    for slot in range(size):
        mask = 0
        for level, distance in enumerate(steps):
            if not (slot >> (len(steps) - 1 - level)) & 1:
                mask ^= distance
        order.append(mask)
    return jnp.array(order) ^ me


def col_sum(value):
    size = lax.axis_size("col")
    for distance in spread(size):
        value = value + lax.ppermute(
            value, "col", [(i, i ^ distance) for i in range(size)]
        )
    return value


def scatter_rows(value, size):
    for distance in spread(size):
        count = value.shape[0] // 2
        value = value[count:] + swap(value[:count], distance, size)
    return value


def shards(basis, panel_one, panel_two, gradient):
    size = lax.axis_size("row")
    k = panel_one.shape[1]
    span = panel_one.shape[0]
    lanes = gradient.shape[1] // size
    me = lax.axis_index("row")
    own = jnp.concatenate([panel_one, panel_two], axis=1)
    held = {0: own}
    beside = swap(own, 1, size)
    for distance in reversed(spread(size)):
        keys = [key for key in sorted(held) if distance > 1 or key]
        if distance == 1:
            held[1] = beside
        if keys:
            got = swap(jnp.stack([held[key] for key in keys]), distance, size)
            for index, key in enumerate(keys):
                held[key ^ distance] = got[index]
    held = jnp.stack([held[key] for key in range(size)])

    gram_own = inner_rows(own, own)
    gram_chip = gram_own + swap(gram_own, 1, size)
    half = me % 2
    rows = gram_chip.shape[0] // 2
    mine = col_sum(lax.dynamic_slice_in_dim(gram_chip, half * rows, rows, axis=0))
    for distance in spread(size)[1:]:
        mine = mine + swap(mine, distance, size)
    halves = jnp.stack([mine, swap(mine, 1, size)])
    gram = jnp.take(halves, jnp.array([0, 1]) ^ half, axis=0).reshape(2 * rows, -1)

    order = slot_order(me, size)
    shuffled = jnp.take(gradient.reshape(-1, size, lanes), order, axis=1).reshape(gradient.shape)
    head, _ = lax.optimization_barrier((inner_rows(shuffled, basis), held))
    head = scatter_rows(head, size)

    image = None
    for slot in range(size):
        cols = lax.dynamic_slice_in_dim(basis, (me ^ slot) * span, span, axis=1)
        part = dot_high(cols, held[slot])
        image = part if image is None else image + part
    image = col_sum(image)

    gathered = jnp.take(held, jnp.arange(size) ^ me, axis=0).reshape(size * span, -1)
    factor_one = tri_factor_doubling(gram[:k, :k])
    factor_two = tri_factor_doubling(gram[k:, k:])
    first = dot_high(image[:, :k], factor_one)
    image_two = image[:, k:] - dot_high(first, gram[:k, k:])
    second = dot_high(image_two, factor_two)
    weight = jnp.concatenate([first, second], axis=1)
    new_basis = basis - outer_cols(weight, gathered)
    tail = scatter_rows(inner_rows(shuffled, weight), size)
    rotated = head - outer_cols(tail, gathered)
    return (new_basis, rotated)


def solution(mesh):
    return jax.shard_map(
        shards,
        mesh=mesh,
        in_specs=(
            P(("parts", "row"), "col"),
            P(("parts", "col", "row"), None),
            P(("parts", "col", "row"), None),
            P(("parts", "row"), None),
        ),
        out_specs=(P(("parts", "row"), "col"), P(("parts", "row"), "col")),
        check_vma=False,
    )
```

```python
import jax
import jax.numpy as jnp
from jax import lax
from jax.sharding import PartitionSpec as P


def dot_high(left, right):
    return jnp.dot(left, right, precision=lax.Precision.HIGHEST, preferred_element_type=jnp.float32)


def inner_rows(left, right):
    return jnp.einsum(
        "ra,rb->ab",
        left,
        right,
        precision=lax.Precision.HIGHEST,
        preferred_element_type=jnp.float32,
    )


def outer_cols(left, right):
    return jnp.einsum(
        "rk,ck->rc",
        left,
        right,
        precision=lax.Precision.HIGHEST,
        preferred_element_type=jnp.float32,
    )


def tri_inverse(upper):
    size = upper.shape[0]
    width = 8
    count = size // width
    shaped = upper.reshape(count, width, count, width)
    selector = jnp.eye(count, dtype=upper.dtype)
    blocks = jnp.einsum("iajb,ij->iab", shaped, selector, precision=lax.Precision.HIGHEST)
    inverse = jnp.zeros_like(blocks)
    unit = jnp.eye(width, dtype=upper.dtype)
    for line in range(width - 1, -1, -1):
        known = jnp.einsum(
            "bj,bjc->bc", blocks[:, line, :], inverse, precision=lax.Precision.HIGHEST
        )
        value = (unit[line][None, :] - known) / blocks[:, line, line][:, None]
        inverse = inverse.at[:, line, :].set(value)
    span = width
    while count > 1:
        shaped = upper.reshape(count, span, count, span)
        pairs = count // 2
        lefts = jnp.arange(pairs) * 2
        pick = (
            (jnp.arange(count)[None, :, None] == lefts[:, None, None])
            & (jnp.arange(count)[None, None, :] == lefts[:, None, None] + 1)
        ).astype(upper.dtype)
        corner = jnp.einsum("iajb,pij->pab", shaped, pick, precision=lax.Precision.HIGHEST)
        first = inverse[0::2]
        second = inverse[1::2]
        top = -jnp.einsum(
            "pab,pbc->pac",
            jnp.einsum("pab,pbc->pac", first, corner, precision=lax.Precision.HIGHEST),
            second,
            precision=lax.Precision.HIGHEST,
        )
        upper_half = jnp.concatenate([first, top], axis=2)
        lower_half = jnp.concatenate([jnp.zeros_like(second), second], axis=2)
        inverse = jnp.concatenate([upper_half, lower_half], axis=1)
        count = pairs
        span = span * 2
    return inverse[0]


def tri_factor(gram):
    upper = jnp.triu(gram, 1) + jnp.diag(jnp.diag(gram)) * 0.5
    return tri_inverse(upper)


def tri_factor_doubling(gram):
    size = gram.shape[0]
    upper = jnp.triu(gram, 1) + jnp.diag(jnp.diag(gram)) * 0.5
    index = jnp.arange(size)
    same = index[:, None] == index[None, :]
    inverse = jnp.where(same, 1.0 / jnp.diag(upper)[None, :], 0.0)
    span = 1
    while span < size:
        group = index // (2 * span)
        side = (index // span) % 2
        corner = (group[:, None] == group[None, :]) & (side[:, None] == 0) & (side[None, :] == 1)
        inverse = inverse - dot_high(dot_high(inverse, jnp.where(corner, upper, 0.0)), inverse)
        span *= 2
    return inverse


def swap(value, distance, size):
    return lax.ppermute(value, "row", [(i, i ^ distance) for i in range(size)])


def spread(size):
    steps = []
    distance = 1
    while distance < size:
        steps.append(distance)
        distance *= 2
    return steps


def slot_order(me, size):
    steps = spread(size)
    order = []
    for slot in range(size):
        mask = 0
        for level, distance in enumerate(steps):
            if not (slot >> (len(steps) - 1 - level)) & 1:
                mask ^= distance
        order.append(mask)
    return jnp.array(order) ^ me


def col_sum(value):
    size = lax.axis_size("col")
    for distance in spread(size):
        value = value + lax.ppermute(
            value, "col", [(i, i ^ distance) for i in range(size)]
        )
    return value


def scatter_rows(value, size):
    for distance in spread(size):
        count = value.shape[0] // 2
        value = value[count:] + swap(value[:count], distance, size)
    return value


def shards(basis, panel_one, panel_two, gradient):
    size = lax.axis_size("row")
    k = panel_one.shape[1]
    span = panel_one.shape[0]
    lanes = gradient.shape[1] // size
    me = lax.axis_index("row")
    own = jnp.concatenate([panel_one, panel_two], axis=1)
    held = {0: own}
    beside = swap(own, 1, size)
    landed = own
    for distance in reversed(spread(size)):
        keys = [key for key in sorted(held) if distance > 1 or key]
        if distance == 1:
            held[1] = beside
        if keys:
            got = swap(jnp.stack([held[key] for key in keys]), distance, size)
            if distance > 1:
                landed = got
            for index, key in enumerate(keys):
                held[key ^ distance] = got[index]
    held = jnp.stack([held[key] for key in range(size)])

    order = slot_order(me, size)
    shuffled = jnp.take(gradient.reshape(-1, size, lanes), order, axis=1).reshape(gradient.shape)
    head = inner_rows(shuffled, basis)
    count = head.shape[0] // 2
    head = head[count:] + swap(head[:count], 1, size)

    gram_own = inner_rows(own, own)
    gram_chip = gram_own + swap(gram_own, 1, size)
    half = me % 2
    rows = gram_chip.shape[0] // 2
    mine = col_sum(lax.dynamic_slice_in_dim(gram_chip, half * rows, rows, axis=0))
    mine, head = lax.optimization_barrier((mine, head))
    for distance in spread(size)[1:]:
        mine = mine + swap(mine, distance, size)
    halves = jnp.stack([mine, swap(mine, 1, size)])
    gram = jnp.take(halves, jnp.array([0, 1]) ^ half, axis=0).reshape(2 * rows, -1)

    head, _ = lax.optimization_barrier((head, landed))
    for distance in spread(size)[1:]:
        count = head.shape[0] // 2
        head = head[count:] + swap(head[:count], distance, size)

    image = None
    for slot in range(size):
        cols = lax.dynamic_slice_in_dim(basis, (me ^ slot) * span, span, axis=1)
        part = dot_high(cols, held[slot])
        image = part if image is None else image + part
    image = col_sum(image)

    gathered = jnp.take(held, jnp.arange(size) ^ me, axis=0).reshape(size * span, -1)
    factor_one = tri_factor_doubling(gram[:k, :k])
    factor_two = tri_factor_doubling(gram[k:, k:])
    first = dot_high(image[:, :k], factor_one)
    image_two = image[:, k:] - dot_high(first, gram[:k, k:])
    second = dot_high(image_two, factor_two)
    weight = jnp.concatenate([first, second], axis=1)
    new_basis = basis - outer_cols(weight, gathered)
    tail = scatter_rows(inner_rows(shuffled, weight), size)
    rotated = head - outer_cols(tail, gathered)
    return (new_basis, rotated)


def solution(mesh):
    return jax.shard_map(
        shards,
        mesh=mesh,
        in_specs=(
            P(("parts", "row"), "col"),
            P(("parts", "col", "row"), None),
            P(("parts", "col", "row"), None),
            P(("parts", "row"), None),
        ),
        out_specs=(P(("parts", "row"), "col"), P(("parts", "row"), "col")),
        check_vma=False,
    )
```

```python
import jax
import jax.numpy as jnp
from jax import lax
from jax.sharding import PartitionSpec as P


def dot_high(left, right):
    return jnp.dot(left, right, precision=lax.Precision.HIGHEST, preferred_element_type=jnp.float32)


def inner_rows(left, right):
    return jnp.einsum(
        "ra,rb->ab",
        left,
        right,
        precision=lax.Precision.HIGHEST,
        preferred_element_type=jnp.float32,
    )


def outer_cols(left, right):
    return jnp.einsum(
        "rk,ck->rc",
        left,
        right,
        precision=lax.Precision.HIGHEST,
        preferred_element_type=jnp.float32,
    )


def tri_inverse(upper):
    size = upper.shape[0]
    width = 8
    count = size // width
    shaped = upper.reshape(count, width, count, width)
    selector = jnp.eye(count, dtype=upper.dtype)
    blocks = jnp.einsum("iajb,ij->iab", shaped, selector, precision=lax.Precision.HIGHEST)
    inverse = jnp.zeros_like(blocks)
    unit = jnp.eye(width, dtype=upper.dtype)
    for line in range(width - 1, -1, -1):
        known = jnp.einsum(
            "bj,bjc->bc", blocks[:, line, :], inverse, precision=lax.Precision.HIGHEST
        )
        value = (unit[line][None, :] - known) / blocks[:, line, line][:, None]
        inverse = inverse.at[:, line, :].set(value)
    span = width
    while count > 1:
        shaped = upper.reshape(count, span, count, span)
        pairs = count // 2
        lefts = jnp.arange(pairs) * 2
        pick = (
            (jnp.arange(count)[None, :, None] == lefts[:, None, None])
            & (jnp.arange(count)[None, None, :] == lefts[:, None, None] + 1)
        ).astype(upper.dtype)
        corner = jnp.einsum("iajb,pij->pab", shaped, pick, precision=lax.Precision.HIGHEST)
        first = inverse[0::2]
        second = inverse[1::2]
        top = -jnp.einsum(
            "pab,pbc->pac",
            jnp.einsum("pab,pbc->pac", first, corner, precision=lax.Precision.HIGHEST),
            second,
            precision=lax.Precision.HIGHEST,
        )
        upper_half = jnp.concatenate([first, top], axis=2)
        lower_half = jnp.concatenate([jnp.zeros_like(second), second], axis=2)
        inverse = jnp.concatenate([upper_half, lower_half], axis=1)
        count = pairs
        span = span * 2
    return inverse[0]


def tri_factor(gram):
    upper = jnp.triu(gram, 1) + jnp.diag(jnp.diag(gram)) * 0.5
    return tri_inverse(upper)


def tri_factor_doubling(gram):
    size = gram.shape[0]
    upper = jnp.triu(gram, 1) + jnp.diag(jnp.diag(gram)) * 0.5
    index = jnp.arange(size)
    same = index[:, None] == index[None, :]
    inverse = jnp.where(same, 1.0 / jnp.diag(upper)[None, :], 0.0)
    span = 1
    while span < size:
        group = index // (2 * span)
        side = (index // span) % 2
        corner = (group[:, None] == group[None, :]) & (side[:, None] == 0) & (side[None, :] == 1)
        inverse = inverse - dot_high(dot_high(inverse, jnp.where(corner, upper, 0.0)), inverse)
        span *= 2
    return inverse


def swap(value, distance, size):
    return lax.ppermute(value, "row", [(i, i ^ distance) for i in range(size)])


def spread(size):
    steps = []
    distance = 1
    while distance < size:
        steps.append(distance)
        distance *= 2
    return steps


def slot_order(me, size):
    steps = spread(size)
    order = []
    for slot in range(size):
        mask = 0
        for level, distance in enumerate(steps):
            if not (slot >> (len(steps) - 1 - level)) & 1:
                mask ^= distance
        order.append(mask)
    return jnp.array(order) ^ me


def col_sum(value):
    size = lax.axis_size("col")
    for distance in spread(size):
        value = value + lax.ppermute(
            value, "col", [(i, i ^ distance) for i in range(size)]
        )
    return value


def scatter_rows(value, size):
    for distance in spread(size):
        count = value.shape[0] // 2
        value = value[count:] + swap(value[:count], distance, size)
    return value


def shards(basis, panel_one, panel_two, gradient):
    size = lax.axis_size("row")
    k = panel_one.shape[1]
    span = panel_one.shape[0]
    lanes = gradient.shape[1] // size
    me = lax.axis_index("row")
    own = jnp.concatenate([panel_one, panel_two], axis=1)
    held = {0: own}
    beside = swap(own, 1, size)
    landed = own
    for distance in reversed(spread(size)):
        keys = [key for key in sorted(held) if distance > 1 or key]
        if distance == 1:
            held[1] = beside
        if keys:
            got = swap(jnp.stack([held[key] for key in keys]), distance, size)
            if distance > 1:
                landed = got
            for index, key in enumerate(keys):
                held[key ^ distance] = got[index]
    held = jnp.stack([held[key] for key in range(size)])

    order = slot_order(me, size)
    shuffled = jnp.take(gradient.reshape(-1, size, lanes), order, axis=1).reshape(gradient.shape)
    head = inner_rows(shuffled, basis)
    count = head.shape[0] // 2
    head = head[count:] + swap(head[:count], 1, size)

    gram_own = inner_rows(own, own)
    gram_chip = gram_own + swap(gram_own, 1, size)
    half = me % 2
    rows = gram_chip.shape[0] // 2
    mine = col_sum(lax.dynamic_slice_in_dim(gram_chip, half * rows, rows, axis=0))
    mine, head = lax.optimization_barrier((mine, head))
    for distance in spread(size)[1:]:
        mine = mine + swap(mine, distance, size)
    block = lax.dynamic_slice_in_dim(mine, half * rows, rows, axis=1)
    cross = jnp.where(half == 0, mine[:, rows:], mine[:, :rows].T)

    head, _ = lax.optimization_barrier((head, landed))
    for distance in spread(size)[1:]:
        count = head.shape[0] // 2
        head = head[count:] + swap(head[:count], distance, size)

    image = None
    for slot in range(size):
        cols = lax.dynamic_slice_in_dim(basis, (me ^ slot) * span, span, axis=1)
        part = dot_high(cols, held[slot])
        image = part if image is None else image + part
    image = col_sum(image)

    gathered = jnp.take(held, jnp.arange(size) ^ me, axis=0).reshape(size * span, -1)
    factor_mine = tri_factor_doubling(block)
    factors = jnp.stack([factor_mine, swap(factor_mine, 1, size)])
    factor_one = jnp.take(factors, half, axis=0)
    factor_two = jnp.take(factors, 1 - half, axis=0)
    first = dot_high(image[:, :k], factor_one)
    image_two = image[:, k:] - dot_high(first, cross)
    second = dot_high(image_two, factor_two)
    weight = jnp.concatenate([first, second], axis=1)
    new_basis = basis - outer_cols(weight, gathered)
    tail = scatter_rows(inner_rows(shuffled, weight), size)
    rotated = head - outer_cols(tail, gathered)
    return (new_basis, rotated)


def solution(mesh):
    return jax.shard_map(
        shards,
        mesh=mesh,
        in_specs=(
            P(("parts", "row"), "col"),
            P(("parts", "col", "row"), None),
            P(("parts", "col", "row"), None),
            P(("parts", "row"), None),
        ),
        out_specs=(P(("parts", "row"), "col"), P(("parts", "row"), "col")),
        check_vma=False,
    )
```

```python
import jax
import jax.numpy as jnp
from jax import lax
from jax.sharding import PartitionSpec as P


def dot_high(left, right):
    return jnp.dot(left, right, precision=lax.Precision.HIGHEST, preferred_element_type=jnp.float32)


def inner_rows(left, right):
    return jnp.einsum(
        "ra,rb->ab",
        left,
        right,
        precision=lax.Precision.HIGHEST,
        preferred_element_type=jnp.float32,
    )


def outer_cols(left, right):
    return jnp.einsum(
        "rk,ck->rc",
        left,
        right,
        precision=lax.Precision.HIGHEST,
        preferred_element_type=jnp.float32,
    )


def tri_inverse(upper):
    size = upper.shape[0]
    width = 8
    count = size // width
    shaped = upper.reshape(count, width, count, width)
    selector = jnp.eye(count, dtype=upper.dtype)
    blocks = jnp.einsum("iajb,ij->iab", shaped, selector, precision=lax.Precision.HIGHEST)
    inverse = jnp.zeros_like(blocks)
    unit = jnp.eye(width, dtype=upper.dtype)
    for line in range(width - 1, -1, -1):
        known = jnp.einsum(
            "bj,bjc->bc", blocks[:, line, :], inverse, precision=lax.Precision.HIGHEST
        )
        value = (unit[line][None, :] - known) / blocks[:, line, line][:, None]
        inverse = inverse.at[:, line, :].set(value)
    span = width
    while count > 1:
        shaped = upper.reshape(count, span, count, span)
        pairs = count // 2
        lefts = jnp.arange(pairs) * 2
        pick = (
            (jnp.arange(count)[None, :, None] == lefts[:, None, None])
            & (jnp.arange(count)[None, None, :] == lefts[:, None, None] + 1)
        ).astype(upper.dtype)
        corner = jnp.einsum("iajb,pij->pab", shaped, pick, precision=lax.Precision.HIGHEST)
        first = inverse[0::2]
        second = inverse[1::2]
        top = -jnp.einsum(
            "pab,pbc->pac",
            jnp.einsum("pab,pbc->pac", first, corner, precision=lax.Precision.HIGHEST),
            second,
            precision=lax.Precision.HIGHEST,
        )
        upper_half = jnp.concatenate([first, top], axis=2)
        lower_half = jnp.concatenate([jnp.zeros_like(second), second], axis=2)
        inverse = jnp.concatenate([upper_half, lower_half], axis=1)
        count = pairs
        span = span * 2
    return inverse[0]


def tri_factor(gram):
    upper = jnp.triu(gram, 1) + jnp.diag(jnp.diag(gram)) * 0.5
    return tri_inverse(upper)


def tri_factor_doubling(gram):
    size = gram.shape[0]
    upper = jnp.triu(gram, 1) + jnp.diag(jnp.diag(gram)) * 0.5
    index = jnp.arange(size)
    same = index[:, None] == index[None, :]
    inverse = jnp.where(same, 1.0 / jnp.diag(upper)[None, :], 0.0)
    span = 1
    while span < size:
        group = index // (2 * span)
        side = (index // span) % 2
        corner = (group[:, None] == group[None, :]) & (side[:, None] == 0) & (side[None, :] == 1)
        inverse = inverse - dot_high(dot_high(inverse, jnp.where(corner, upper, 0.0)), inverse)
        span *= 2
    return inverse


def swap(value, distance, size):
    return lax.ppermute(value, "row", [(i, i ^ distance) for i in range(size)])


def spread(size):
    steps = []
    distance = 1
    while distance < size:
        steps.append(distance)
        distance *= 2
    return steps


def slot_order(me, size):
    steps = spread(size)
    order = []
    for slot in range(size):
        mask = 0
        for level, distance in enumerate(steps):
            if not (slot >> (len(steps) - 1 - level)) & 1:
                mask ^= distance
        order.append(mask)
    return jnp.array(order) ^ me


def col_sum(value):
    size = lax.axis_size("col")
    for distance in spread(size):
        value = value + lax.ppermute(
            value, "col", [(i, i ^ distance) for i in range(size)]
        )
    return value


def scatter_rows(value, size):
    for distance in spread(size):
        count = value.shape[0] // 2
        value = value[count:] + swap(value[:count], distance, size)
    return value


def shards(basis, panel_one, panel_two, gradient):
    size = lax.axis_size("row")
    k = panel_one.shape[1]
    span = panel_one.shape[0]
    lanes = gradient.shape[1] // size
    me = lax.axis_index("row")
    own = jnp.concatenate([panel_one, panel_two], axis=1)
    held = {0: own}
    beside = swap(own, 1, size)
    landed = own
    for distance in reversed(spread(size)):
        keys = [key for key in sorted(held) if distance > 1 or key]
        if distance == 1:
            held[1] = beside
        if keys:
            got = swap(jnp.stack([held[key] for key in keys]), distance, size)
            if distance > 1:
                landed = got
            for index, key in enumerate(keys):
                held[key ^ distance] = got[index]
    held = jnp.stack([held[key] for key in range(size)])

    gram_own = inner_rows(own, own)
    gram_chip = gram_own + swap(gram_own, 1, size)
    order = slot_order(me, size)
    shuffled = jnp.take(gradient.reshape(-1, size, lanes), order, axis=1).reshape(gradient.shape)
    shuffled, gram_chip = lax.optimization_barrier((shuffled, gram_chip))
    head = inner_rows(shuffled, basis)
    count = head.shape[0] // 2
    head = head[count:] + swap(head[:count], 1, size)

    half = me % 2
    rows = gram_chip.shape[0] // 2
    mine = col_sum(lax.dynamic_slice_in_dim(gram_chip, half * rows, rows, axis=0))
    mine, head = lax.optimization_barrier((mine, head))
    for distance in spread(size)[1:]:
        mine = mine + swap(mine, distance, size)
    block = lax.dynamic_slice_in_dim(mine, half * rows, rows, axis=1)
    cross = jnp.where(half == 0, mine[:, rows:], mine[:, :rows].T)

    head, _ = lax.optimization_barrier((head, landed))
    for distance in spread(size)[1:]:
        count = head.shape[0] // 2
        head = head[count:] + swap(head[:count], distance, size)

    image = None
    for slot in range(size):
        cols = lax.dynamic_slice_in_dim(basis, (me ^ slot) * span, span, axis=1)
        part = dot_high(cols, held[slot])
        image = part if image is None else image + part
    image = col_sum(image)

    gathered = jnp.take(held, jnp.arange(size) ^ me, axis=0).reshape(size * span, -1)
    factor_mine = tri_factor_doubling(block)
    factors = jnp.stack([factor_mine, swap(factor_mine, 1, size)])
    factor_one = jnp.take(factors, half, axis=0)
    factor_two = jnp.take(factors, 1 - half, axis=0)
    first = dot_high(image[:, :k], factor_one)
    image_two = image[:, k:] - dot_high(first, cross)
    second = dot_high(image_two, factor_two)
    weight = jnp.concatenate([first, second], axis=1)
    new_basis = basis - outer_cols(weight, gathered)
    tail = scatter_rows(inner_rows(shuffled, weight), size)
    rotated = head - outer_cols(tail, gathered)
    return (new_basis, rotated)


def solution(mesh):
    return jax.shard_map(
        shards,
        mesh=mesh,
        in_specs=(
            P(("parts", "row"), "col"),
            P(("parts", "col", "row"), None),
            P(("parts", "col", "row"), None),
            P(("parts", "row"), None),
        ),
        out_specs=(P(("parts", "row"), "col"), P(("parts", "row"), "col")),
        check_vma=False,
    )
```

```python
import jax
import jax.numpy as jnp
from jax import lax
from jax.sharding import PartitionSpec as P


def dot_high(left, right):
    return jnp.dot(left, right, precision=lax.Precision.HIGHEST, preferred_element_type=jnp.float32)


def inner_rows(left, right):
    return jnp.einsum(
        "ra,rb->ab",
        left,
        right,
        precision=lax.Precision.HIGHEST,
        preferred_element_type=jnp.float32,
    )


def outer_cols(left, right):
    return jnp.einsum(
        "rk,ck->rc",
        left,
        right,
        precision=lax.Precision.HIGHEST,
        preferred_element_type=jnp.float32,
    )


def tri_inverse(upper):
    size = upper.shape[0]
    width = 8
    count = size // width
    shaped = upper.reshape(count, width, count, width)
    selector = jnp.eye(count, dtype=upper.dtype)
    blocks = jnp.einsum("iajb,ij->iab", shaped, selector, precision=lax.Precision.HIGHEST)
    inverse = jnp.zeros_like(blocks)
    unit = jnp.eye(width, dtype=upper.dtype)
    for line in range(width - 1, -1, -1):
        known = jnp.einsum(
            "bj,bjc->bc", blocks[:, line, :], inverse, precision=lax.Precision.HIGHEST
        )
        value = (unit[line][None, :] - known) / blocks[:, line, line][:, None]
        inverse = inverse.at[:, line, :].set(value)
    span = width
    while count > 1:
        shaped = upper.reshape(count, span, count, span)
        pairs = count // 2
        lefts = jnp.arange(pairs) * 2
        pick = (
            (jnp.arange(count)[None, :, None] == lefts[:, None, None])
            & (jnp.arange(count)[None, None, :] == lefts[:, None, None] + 1)
        ).astype(upper.dtype)
        corner = jnp.einsum("iajb,pij->pab", shaped, pick, precision=lax.Precision.HIGHEST)
        first = inverse[0::2]
        second = inverse[1::2]
        top = -jnp.einsum(
            "pab,pbc->pac",
            jnp.einsum("pab,pbc->pac", first, corner, precision=lax.Precision.HIGHEST),
            second,
            precision=lax.Precision.HIGHEST,
        )
        upper_half = jnp.concatenate([first, top], axis=2)
        lower_half = jnp.concatenate([jnp.zeros_like(second), second], axis=2)
        inverse = jnp.concatenate([upper_half, lower_half], axis=1)
        count = pairs
        span = span * 2
    return inverse[0]


def tri_factor(gram):
    upper = jnp.triu(gram, 1) + jnp.diag(jnp.diag(gram)) * 0.5
    return tri_inverse(upper)


def tri_factor_doubling(gram):
    size = gram.shape[0]
    upper = jnp.triu(gram, 1) + jnp.diag(jnp.diag(gram)) * 0.5
    index = jnp.arange(size)
    same = index[:, None] == index[None, :]
    inverse = jnp.where(same, 1.0 / jnp.diag(upper)[None, :], 0.0)
    span = 1
    while span < size:
        group = index // (2 * span)
        side = (index // span) % 2
        corner = (group[:, None] == group[None, :]) & (side[:, None] == 0) & (side[None, :] == 1)
        inverse = inverse - dot_high(dot_high(inverse, jnp.where(corner, upper, 0.0)), inverse)
        span *= 2
    return inverse


def swap(value, distance, size):
    return lax.ppermute(value, "row", [(i, i ^ distance) for i in range(size)])


def spread(size):
    steps = []
    distance = 1
    while distance < size:
        steps.append(distance)
        distance *= 2
    return steps


def slot_order(me, size):
    steps = spread(size)
    order = []
    for slot in range(size):
        mask = 0
        for level, distance in enumerate(steps):
            if not (slot >> (len(steps) - 1 - level)) & 1:
                mask ^= distance
        order.append(mask)
    return jnp.array(order) ^ me


def col_sum(value):
    size = lax.axis_size("col")
    for distance in spread(size):
        value = value + lax.ppermute(
            value, "col", [(i, i ^ distance) for i in range(size)]
        )
    return value


def scatter_rows(value, size):
    for distance in spread(size):
        count = value.shape[0] // 2
        value = value[count:] + swap(value[:count], distance, size)
    return value


def shards(basis, panel_one, panel_two, gradient):
    size = lax.axis_size("row")
    k = panel_one.shape[1]
    span = panel_one.shape[0]
    lanes = gradient.shape[1] // size
    me = lax.axis_index("row")
    own = jnp.concatenate([panel_one, panel_two], axis=1)
    held = {0: own}
    beside = swap(own, 1, size)
    landed = own
    for distance in reversed(spread(size)):
        keys = [key for key in sorted(held) if distance > 1 or key]
        if distance == 1:
            held[1] = beside
        if keys:
            got = swap(jnp.stack([held[key] for key in keys]), distance, size)
            if distance > 1:
                landed = got
            for index, key in enumerate(keys):
                held[key ^ distance] = got[index]
    held = jnp.stack([held[key] for key in range(size)])

    order = slot_order(me, size)
    shuffled = jnp.take(gradient.reshape(-1, size, lanes), order, axis=1).reshape(gradient.shape)
    head = inner_rows(shuffled, basis)
    count = head.shape[0] // 2
    head = head[count:] + swap(head[:count], 1, size)

    gram_own = inner_rows(own, own)
    gram_chip = gram_own + swap(gram_own, 1, size)
    half = me % 2
    rows = gram_chip.shape[0] // 2
    mine = col_sum(lax.dynamic_slice_in_dim(gram_chip, half * rows, rows, axis=0))
    mine, head = lax.optimization_barrier((mine, head))
    for distance in spread(size)[1:]:
        mine = mine + swap(mine, distance, size)
    halves = jnp.stack([mine, swap(mine, 1, size)])
    gram = jnp.take(halves, jnp.array([0, 1]) ^ half, axis=0).reshape(2 * rows, -1)

    head, _ = lax.optimization_barrier((head, landed))
    for distance in spread(size)[1:]:
        count = head.shape[0] // 2
        head = head[count:] + swap(head[:count], distance, size)

    image = None
    for slot in range(size):
        cols = lax.dynamic_slice_in_dim(basis, (me ^ slot) * span, span, axis=1)
        part = dot_high(cols, held[slot])
        image = part if image is None else image + part
    image = col_sum(image)

    gathered = jnp.take(held, jnp.arange(size) ^ me, axis=0).reshape(size * span, -1)
    factor_one = tri_factor_doubling(gram[:k, :k])
    factor_two = tri_factor_doubling(gram[k:, k:])
    first = dot_high(image[:, :k], factor_one)
    image_two = image[:, k:] - dot_high(first, gram[:k, k:])
    second = dot_high(image_two, factor_two)
    weight = jnp.concatenate([first, second], axis=1)
    weight, head = lax.optimization_barrier((weight, head))
    new_basis = basis - outer_cols(weight, gathered)
    tail = scatter_rows(inner_rows(shuffled, weight), size)
    rotated = head - outer_cols(tail, gathered)
    return (new_basis, rotated)


def solution(mesh):
    return jax.shard_map(
        shards,
        mesh=mesh,
        in_specs=(
            P(("parts", "row"), "col"),
            P(("parts", "col", "row"), None),
            P(("parts", "col", "row"), None),
            P(("parts", "row"), None),
        ),
        out_specs=(P(("parts", "row"), "col"), P(("parts", "row"), "col")),
        check_vma=False,
    )
```

```python
import jax
import jax.numpy as jnp
from jax import lax
from jax.sharding import PartitionSpec as P


def dot_high(left, right):
    return jnp.dot(left, right, precision=lax.Precision.HIGHEST, preferred_element_type=jnp.float32)


def inner_rows(left, right):
    return jnp.einsum(
        "ra,rb->ab",
        left,
        right,
        precision=lax.Precision.HIGHEST,
        preferred_element_type=jnp.float32,
    )


def outer_cols(left, right):
    return jnp.einsum(
        "rk,ck->rc",
        left,
        right,
        precision=lax.Precision.HIGHEST,
        preferred_element_type=jnp.float32,
    )


def tri_inverse(upper):
    size = upper.shape[0]
    width = 8
    count = size // width
    shaped = upper.reshape(count, width, count, width)
    selector = jnp.eye(count, dtype=upper.dtype)
    blocks = jnp.einsum("iajb,ij->iab", shaped, selector, precision=lax.Precision.HIGHEST)
    inverse = jnp.zeros_like(blocks)
    unit = jnp.eye(width, dtype=upper.dtype)
    for line in range(width - 1, -1, -1):
        known = jnp.einsum(
            "bj,bjc->bc", blocks[:, line, :], inverse, precision=lax.Precision.HIGHEST
        )
        value = (unit[line][None, :] - known) / blocks[:, line, line][:, None]
        inverse = inverse.at[:, line, :].set(value)
    span = width
    while count > 1:
        shaped = upper.reshape(count, span, count, span)
        pairs = count // 2
        lefts = jnp.arange(pairs) * 2
        pick = (
            (jnp.arange(count)[None, :, None] == lefts[:, None, None])
            & (jnp.arange(count)[None, None, :] == lefts[:, None, None] + 1)
        ).astype(upper.dtype)
        corner = jnp.einsum("iajb,pij->pab", shaped, pick, precision=lax.Precision.HIGHEST)
        first = inverse[0::2]
        second = inverse[1::2]
        top = -jnp.einsum(
            "pab,pbc->pac",
            jnp.einsum("pab,pbc->pac", first, corner, precision=lax.Precision.HIGHEST),
            second,
            precision=lax.Precision.HIGHEST,
        )
        upper_half = jnp.concatenate([first, top], axis=2)
        lower_half = jnp.concatenate([jnp.zeros_like(second), second], axis=2)
        inverse = jnp.concatenate([upper_half, lower_half], axis=1)
        count = pairs
        span = span * 2
    return inverse[0]


def tri_factor(gram):
    upper = jnp.triu(gram, 1) + jnp.diag(jnp.diag(gram)) * 0.5
    return tri_inverse(upper)


def tri_factor_doubling(gram):
    size = gram.shape[0]
    upper = jnp.triu(gram, 1) + jnp.diag(jnp.diag(gram)) * 0.5
    index = jnp.arange(size)
    same = index[:, None] == index[None, :]
    inverse = jnp.where(same, 1.0 / jnp.diag(upper)[None, :], 0.0)
    span = 1
    while span < size:
        group = index // (2 * span)
        side = (index // span) % 2
        corner = (group[:, None] == group[None, :]) & (side[:, None] == 0) & (side[None, :] == 1)
        inverse = inverse - dot_high(dot_high(inverse, jnp.where(corner, upper, 0.0)), inverse)
        span *= 2
    return inverse


def swap(value, distance, size):
    return lax.ppermute(value, "row", [(i, i ^ distance) for i in range(size)])


def spread(size):
    steps = []
    distance = 1
    while distance < size:
        steps.append(distance)
        distance *= 2
    return steps


def slot_order(me, size):
    steps = spread(size)
    order = []
    for slot in range(size):
        mask = 0
        for level, distance in enumerate(steps):
            if not (slot >> (len(steps) - 1 - level)) & 1:
                mask ^= distance
        order.append(mask)
    return jnp.array(order) ^ me


def col_sum(value):
    size = lax.axis_size("col")
    for distance in spread(size):
        value = value + lax.ppermute(
            value, "col", [(i, i ^ distance) for i in range(size)]
        )
    return value


def col_sum_split(value):
    size = lax.axis_size("col")
    me = lax.axis_index("col")
    steps = spread(size)
    pairs = lambda distance: [(i, i ^ distance) for i in range(size)]
    for distance in steps:
        bit = (me // distance) % 2
        count = value.shape[0] // 2
        keep = lax.dynamic_slice_in_dim(value, bit * count, count, axis=0)
        send = lax.dynamic_slice_in_dim(value, (1 - bit) * count, count, axis=0)
        value = keep + lax.ppermute(send, "col", pairs(distance))
    for distance in reversed(steps):
        bit = (me // distance) % 2
        other = lax.ppermute(value, "col", pairs(distance))
        value = jnp.concatenate(
            [jnp.where(bit == 0, value, other), jnp.where(bit == 0, other, value)], axis=0
        )
    return value


def scatter_rows(value, size):
    for distance in spread(size):
        count = value.shape[0] // 2
        value = value[count:] + swap(value[:count], distance, size)
    return value


def shards(basis, panel_one, panel_two, gradient):
    size = lax.axis_size("row")
    k = panel_one.shape[1]
    span = panel_one.shape[0]
    lanes = gradient.shape[1] // size
    me = lax.axis_index("row")
    own = jnp.concatenate([panel_one, panel_two], axis=1)
    held = {0: own}
    beside = swap(own, 1, size)
    landed = own
    for distance in reversed(spread(size)):
        keys = [key for key in sorted(held) if distance > 1 or key]
        if distance == 1:
            held[1] = beside
        if keys:
            got = swap(jnp.stack([held[key] for key in keys]), distance, size)
            if distance > 1:
                landed = got
            for index, key in enumerate(keys):
                held[key ^ distance] = got[index]
    held = jnp.stack([held[key] for key in range(size)])

    order = slot_order(me, size)
    shuffled = jnp.take(gradient.reshape(-1, size, lanes), order, axis=1).reshape(gradient.shape)
    head = inner_rows(shuffled, basis)
    count = head.shape[0] // 2
    head = head[count:] + swap(head[:count], 1, size)

    gram_own = inner_rows(own, own)
    gram_chip = gram_own + swap(gram_own, 1, size)
    half = me % 2
    rows = gram_chip.shape[0] // 2
    mine = col_sum(lax.dynamic_slice_in_dim(gram_chip, half * rows, rows, axis=0))
    mine, head = lax.optimization_barrier((mine, head))
    for distance in spread(size)[1:]:
        mine = mine + swap(mine, distance, size)
    halves = jnp.stack([mine, swap(mine, 1, size)])
    gram = jnp.take(halves, jnp.array([0, 1]) ^ half, axis=0).reshape(2 * rows, -1)

    head, _ = lax.optimization_barrier((head, landed))
    for distance in spread(size)[1:]:
        count = head.shape[0] // 2
        head = head[count:] + swap(head[:count], distance, size)

    image = None
    for slot in range(size):
        cols = lax.dynamic_slice_in_dim(basis, (me ^ slot) * span, span, axis=1)
        part = dot_high(cols, held[slot])
        image = part if image is None else image + part
    image = col_sum_split(image)

    gathered = jnp.take(held, jnp.arange(size) ^ me, axis=0).reshape(size * span, -1)
    factor_one = tri_factor_doubling(gram[:k, :k])
    factor_two = tri_factor_doubling(gram[k:, k:])
    first = dot_high(image[:, :k], factor_one)
    image_two = image[:, k:] - dot_high(first, gram[:k, k:])
    second = dot_high(image_two, factor_two)
    weight = jnp.concatenate([first, second], axis=1)
    new_basis = basis - outer_cols(weight, gathered)
    tail = scatter_rows(inner_rows(shuffled, weight), size)
    rotated = head - outer_cols(tail, gathered)
    return (new_basis, rotated)


def solution(mesh):
    return jax.shard_map(
        shards,
        mesh=mesh,
        in_specs=(
            P(("parts", "row"), "col"),
            P(("parts", "col", "row"), None),
            P(("parts", "col", "row"), None),
            P(("parts", "row"), None),
        ),
        out_specs=(P(("parts", "row"), "col"), P(("parts", "row"), "col")),
        check_vma=False,
    )
```

```python
import jax
import jax.numpy as jnp
from jax import lax
from jax.sharding import PartitionSpec as P


def dot_high(left, right):
    return jnp.dot(left, right, precision=lax.Precision.HIGHEST, preferred_element_type=jnp.float32)


def inner_rows(left, right):
    return jnp.einsum(
        "ra,rb->ab",
        left,
        right,
        precision=lax.Precision.HIGHEST,
        preferred_element_type=jnp.float32,
    )


def outer_cols(left, right):
    return jnp.einsum(
        "rk,ck->rc",
        left,
        right,
        precision=lax.Precision.HIGHEST,
        preferred_element_type=jnp.float32,
    )


def outer_mid(left, right):
    return jnp.einsum(
        "rk,ck->rc",
        left,
        right,
        precision=lax.Precision.HIGH,
        preferred_element_type=jnp.float32,
    )


def inner_mid(left, right):
    return jnp.einsum(
        "ra,rb->ab",
        left,
        right,
        precision=lax.Precision.HIGH,
        preferred_element_type=jnp.float32,
    )


def tri_inverse(upper):
    size = upper.shape[0]
    width = 8
    count = size // width
    shaped = upper.reshape(count, width, count, width)
    selector = jnp.eye(count, dtype=upper.dtype)
    blocks = jnp.einsum("iajb,ij->iab", shaped, selector, precision=lax.Precision.HIGHEST)
    inverse = jnp.zeros_like(blocks)
    unit = jnp.eye(width, dtype=upper.dtype)
    for line in range(width - 1, -1, -1):
        known = jnp.einsum(
            "bj,bjc->bc", blocks[:, line, :], inverse, precision=lax.Precision.HIGHEST
        )
        value = (unit[line][None, :] - known) / blocks[:, line, line][:, None]
        inverse = inverse.at[:, line, :].set(value)
    span = width
    while count > 1:
        shaped = upper.reshape(count, span, count, span)
        pairs = count // 2
        lefts = jnp.arange(pairs) * 2
        pick = (
            (jnp.arange(count)[None, :, None] == lefts[:, None, None])
            & (jnp.arange(count)[None, None, :] == lefts[:, None, None] + 1)
        ).astype(upper.dtype)
        corner = jnp.einsum("iajb,pij->pab", shaped, pick, precision=lax.Precision.HIGHEST)
        first = inverse[0::2]
        second = inverse[1::2]
        top = -jnp.einsum(
            "pab,pbc->pac",
            jnp.einsum("pab,pbc->pac", first, corner, precision=lax.Precision.HIGHEST),
            second,
            precision=lax.Precision.HIGHEST,
        )
        upper_half = jnp.concatenate([first, top], axis=2)
        lower_half = jnp.concatenate([jnp.zeros_like(second), second], axis=2)
        inverse = jnp.concatenate([upper_half, lower_half], axis=1)
        count = pairs
        span = span * 2
    return inverse[0]


def tri_factor(gram):
    upper = jnp.triu(gram, 1) + jnp.diag(jnp.diag(gram)) * 0.5
    return tri_inverse(upper)


def tri_factor_doubling(gram):
    size = gram.shape[0]
    upper = jnp.triu(gram, 1) + jnp.diag(jnp.diag(gram)) * 0.5
    index = jnp.arange(size)
    same = index[:, None] == index[None, :]
    inverse = jnp.where(same, 1.0 / jnp.diag(upper)[None, :], 0.0)
    span = 1
    while span < size:
        group = index // (2 * span)
        side = (index // span) % 2
        corner = (group[:, None] == group[None, :]) & (side[:, None] == 0) & (side[None, :] == 1)
        inverse = inverse - dot_high(dot_high(inverse, jnp.where(corner, upper, 0.0)), inverse)
        span *= 2
    return inverse


def swap(value, distance, size):
    return lax.ppermute(value, "row", [(i, i ^ distance) for i in range(size)])


def spread(size):
    steps = []
    distance = 1
    while distance < size:
        steps.append(distance)
        distance *= 2
    return steps


def slot_order(me, size):
    steps = spread(size)
    order = []
    for slot in range(size):
        mask = 0
        for level, distance in enumerate(steps):
            if not (slot >> (len(steps) - 1 - level)) & 1:
                mask ^= distance
        order.append(mask)
    return jnp.array(order) ^ me


def col_sum(value):
    size = lax.axis_size("col")
    for distance in spread(size):
        value = value + lax.ppermute(
            value, "col", [(i, i ^ distance) for i in range(size)]
        )
    return value


def scatter_rows(value, size):
    for distance in spread(size):
        count = value.shape[0] // 2
        value = value[count:] + swap(value[:count], distance, size)
    return value


def shards(basis, panel_one, panel_two, gradient):
    size = lax.axis_size("row")
    k = panel_one.shape[1]
    span = panel_one.shape[0]
    lanes = gradient.shape[1] // size
    me = lax.axis_index("row")
    own = jnp.concatenate([panel_one, panel_two], axis=1)
    held = {0: own}
    beside = swap(own, 1, size)
    landed = own
    for distance in reversed(spread(size)):
        keys = [key for key in sorted(held) if distance > 1 or key]
        if distance == 1:
            held[1] = beside
        if keys:
            got = swap(jnp.stack([held[key] for key in keys]), distance, size)
            if distance > 1:
                landed = got
            for index, key in enumerate(keys):
                held[key ^ distance] = got[index]
    held = jnp.stack([held[key] for key in range(size)])

    order = slot_order(me, size)
    shuffled = jnp.take(gradient.reshape(-1, size, lanes), order, axis=1).reshape(gradient.shape)
    head = inner_mid(shuffled, basis)
    count = head.shape[0] // 2
    head = head[count:] + swap(head[:count], 1, size)

    gram_own = inner_rows(own, own)
    gram_chip = gram_own + swap(gram_own, 1, size)
    half = me % 2
    rows = gram_chip.shape[0] // 2
    mine = col_sum(lax.dynamic_slice_in_dim(gram_chip, half * rows, rows, axis=0))
    mine, head = lax.optimization_barrier((mine, head))
    for distance in spread(size)[1:]:
        mine = mine + swap(mine, distance, size)
    halves = jnp.stack([mine, swap(mine, 1, size)])
    gram = jnp.take(halves, jnp.array([0, 1]) ^ half, axis=0).reshape(2 * rows, -1)

    head, _ = lax.optimization_barrier((head, landed))
    for distance in spread(size)[1:]:
        count = head.shape[0] // 2
        head = head[count:] + swap(head[:count], distance, size)

    image = None
    for slot in range(size):
        cols = lax.dynamic_slice_in_dim(basis, (me ^ slot) * span, span, axis=1)
        part = dot_high(cols, held[slot])
        image = part if image is None else image + part
    image = col_sum(image)

    gathered = jnp.take(held, jnp.arange(size) ^ me, axis=0).reshape(size * span, -1)
    factor_one = tri_factor_doubling(gram[:k, :k])
    factor_two = tri_factor_doubling(gram[k:, k:])
    first = dot_high(image[:, :k], factor_one)
    image_two = image[:, k:] - dot_high(first, gram[:k, k:])
    second = dot_high(image_two, factor_two)
    weight = jnp.concatenate([first, second], axis=1)
    new_basis = basis - outer_mid(weight, gathered)
    tail = scatter_rows(inner_rows(shuffled, weight), size)
    rotated = head - outer_mid(tail, gathered)
    return (new_basis, rotated)


def solution(mesh):
    return jax.shard_map(
        shards,
        mesh=mesh,
        in_specs=(
            P(("parts", "row"), "col"),
            P(("parts", "col", "row"), None),
            P(("parts", "col", "row"), None),
            P(("parts", "row"), None),
        ),
        out_specs=(P(("parts", "row"), "col"), P(("parts", "row"), "col")),
        check_vma=False,
    )
```

```python
import jax
import jax.numpy as jnp
from jax import lax
from jax.sharding import PartitionSpec as P


def dot_high(left, right):
    return jnp.dot(left, right, precision=lax.Precision.HIGHEST, preferred_element_type=jnp.float32)


def inner_rows(left, right):
    return jnp.einsum(
        "ra,rb->ab",
        left,
        right,
        precision=lax.Precision.HIGHEST,
        preferred_element_type=jnp.float32,
    )


def outer_cols(left, right):
    return jnp.einsum(
        "rk,ck->rc",
        left,
        right,
        precision=lax.Precision.HIGHEST,
        preferred_element_type=jnp.float32,
    )


def outer_mid(left, right):
    return jnp.einsum(
        "rk,ck->rc",
        left,
        right,
        precision=lax.Precision.HIGH,
        preferred_element_type=jnp.float32,
    )


def inner_mid(left, right):
    return jnp.einsum(
        "ra,rb->ab",
        left,
        right,
        precision=lax.Precision.HIGH,
        preferred_element_type=jnp.float32,
    )


def tri_inverse(upper):
    size = upper.shape[0]
    width = 8
    count = size // width
    shaped = upper.reshape(count, width, count, width)
    selector = jnp.eye(count, dtype=upper.dtype)
    blocks = jnp.einsum("iajb,ij->iab", shaped, selector, precision=lax.Precision.HIGHEST)
    inverse = jnp.zeros_like(blocks)
    unit = jnp.eye(width, dtype=upper.dtype)
    for line in range(width - 1, -1, -1):
        known = jnp.einsum(
            "bj,bjc->bc", blocks[:, line, :], inverse, precision=lax.Precision.HIGHEST
        )
        value = (unit[line][None, :] - known) / blocks[:, line, line][:, None]
        inverse = inverse.at[:, line, :].set(value)
    span = width
    while count > 1:
        shaped = upper.reshape(count, span, count, span)
        pairs = count // 2
        lefts = jnp.arange(pairs) * 2
        pick = (
            (jnp.arange(count)[None, :, None] == lefts[:, None, None])
            & (jnp.arange(count)[None, None, :] == lefts[:, None, None] + 1)
        ).astype(upper.dtype)
        corner = jnp.einsum("iajb,pij->pab", shaped, pick, precision=lax.Precision.HIGHEST)
        first = inverse[0::2]
        second = inverse[1::2]
        top = -jnp.einsum(
            "pab,pbc->pac",
            jnp.einsum("pab,pbc->pac", first, corner, precision=lax.Precision.HIGHEST),
            second,
            precision=lax.Precision.HIGHEST,
        )
        upper_half = jnp.concatenate([first, top], axis=2)
        lower_half = jnp.concatenate([jnp.zeros_like(second), second], axis=2)
        inverse = jnp.concatenate([upper_half, lower_half], axis=1)
        count = pairs
        span = span * 2
    return inverse[0]


def tri_factor(gram):
    upper = jnp.triu(gram, 1) + jnp.diag(jnp.diag(gram)) * 0.5
    return tri_inverse(upper)


def tri_factor_doubling(gram):
    size = gram.shape[0]
    upper = jnp.triu(gram, 1) + jnp.diag(jnp.diag(gram)) * 0.5
    index = jnp.arange(size)
    same = index[:, None] == index[None, :]
    inverse = jnp.where(same, 1.0 / jnp.diag(upper)[None, :], 0.0)
    span = 1
    while span < size:
        group = index // (2 * span)
        side = (index // span) % 2
        corner = (group[:, None] == group[None, :]) & (side[:, None] == 0) & (side[None, :] == 1)
        inverse = inverse - dot_high(dot_high(inverse, jnp.where(corner, upper, 0.0)), inverse)
        span *= 2
    return inverse


def swap(value, distance, size):
    return lax.ppermute(value, "row", [(i, i ^ distance) for i in range(size)])


def spread(size):
    steps = []
    distance = 1
    while distance < size:
        steps.append(distance)
        distance *= 2
    return steps


def slot_order(me, size):
    steps = spread(size)
    order = []
    for slot in range(size):
        mask = 0
        for level, distance in enumerate(steps):
            if not (slot >> (len(steps) - 1 - level)) & 1:
                mask ^= distance
        order.append(mask)
    return jnp.array(order) ^ me


def col_sum(value):
    size = lax.axis_size("col")
    for distance in spread(size):
        value = value + lax.ppermute(
            value, "col", [(i, i ^ distance) for i in range(size)]
        )
    return value


def scatter_rows(value, size):
    for distance in spread(size):
        count = value.shape[0] // 2
        value = value[count:] + swap(value[:count], distance, size)
    return value


def shards(basis, panel_one, panel_two, gradient):
    size = lax.axis_size("row")
    k = panel_one.shape[1]
    span = panel_one.shape[0]
    lanes = gradient.shape[1] // size
    me = lax.axis_index("row")
    own = jnp.concatenate([panel_one, panel_two], axis=1)
    held = {0: own}
    beside = swap(own, 1, size)
    landed = own
    for distance in reversed(spread(size)):
        keys = [key for key in sorted(held) if distance > 1 or key]
        if distance == 1:
            held[1] = beside
        if keys:
            got = swap(jnp.stack([held[key] for key in keys]), distance, size)
            if distance > 1:
                landed = got
            for index, key in enumerate(keys):
                held[key ^ distance] = got[index]
    held = jnp.stack([held[key] for key in range(size)])

    order = slot_order(me, size)
    shuffled = jnp.take(gradient.reshape(-1, size, lanes), order, axis=1).reshape(gradient.shape)
    head = inner_mid(shuffled, basis)
    count = head.shape[0] // 2
    head = head[count:] + swap(head[:count], 1, size)

    gram_own = inner_rows(own, own)
    gram_chip = gram_own + swap(gram_own, 1, size)
    half = me % 2
    rows = gram_chip.shape[0] // 2
    mine = col_sum(lax.dynamic_slice_in_dim(gram_chip, half * rows, rows, axis=0))
    mine, head = lax.optimization_barrier((mine, head))
    for distance in spread(size)[1:]:
        mine = mine + swap(mine, distance, size)
    halves = jnp.stack([mine, swap(mine, 1, size)])
    gram = jnp.take(halves, jnp.array([0, 1]) ^ half, axis=0).reshape(2 * rows, -1)

    head, _ = lax.optimization_barrier((head, landed))
    for distance in spread(size)[1:]:
        count = head.shape[0] // 2
        head = head[count:] + swap(head[:count], distance, size)

    image = None
    for slot in range(size):
        cols = lax.dynamic_slice_in_dim(basis, (me ^ slot) * span, span, axis=1)
        part = jnp.dot(cols, held[slot], precision=lax.Precision.HIGH, preferred_element_type=jnp.float32)
        image = part if image is None else image + part
    image = col_sum(image)

    gathered = jnp.take(held, jnp.arange(size) ^ me, axis=0).reshape(size * span, -1)
    factor_one = tri_factor_doubling(gram[:k, :k])
    factor_two = tri_factor_doubling(gram[k:, k:])
    first = dot_high(image[:, :k], factor_one)
    image_two = image[:, k:] - dot_high(first, gram[:k, k:])
    second = dot_high(image_two, factor_two)
    weight = jnp.concatenate([first, second], axis=1)
    new_basis = basis - outer_mid(weight, gathered)
    tail = scatter_rows(inner_rows(shuffled, weight), size)
    rotated = head - outer_mid(tail, gathered)
    return (new_basis, rotated)


def solution(mesh):
    return jax.shard_map(
        shards,
        mesh=mesh,
        in_specs=(
            P(("parts", "row"), "col"),
            P(("parts", "col", "row"), None),
            P(("parts", "col", "row"), None),
            P(("parts", "row"), None),
        ),
        out_specs=(P(("parts", "row"), "col"), P(("parts", "row"), "col")),
        check_vma=False,
    )
```

```python
import jax
import jax.numpy as jnp
from jax import lax
from jax.sharding import PartitionSpec as P


def dot_high(left, right):
    return jnp.dot(left, right, precision=lax.Precision.HIGHEST, preferred_element_type=jnp.float32)


def inner_rows(left, right):
    return jnp.einsum(
        "ra,rb->ab",
        left,
        right,
        precision=lax.Precision.HIGHEST,
        preferred_element_type=jnp.float32,
    )


def outer_cols(left, right):
    return jnp.einsum(
        "rk,ck->rc",
        left,
        right,
        precision=lax.Precision.HIGHEST,
        preferred_element_type=jnp.float32,
    )


def outer_mid(left, right):
    return jnp.einsum(
        "rk,ck->rc",
        left,
        right,
        precision=lax.Precision.HIGH,
        preferred_element_type=jnp.float32,
    )


def inner_mid(left, right):
    return jnp.einsum(
        "ra,rb->ab",
        left,
        right,
        precision=lax.Precision.HIGH,
        preferred_element_type=jnp.float32,
    )


def tri_inverse(upper):
    size = upper.shape[0]
    width = 8
    count = size // width
    shaped = upper.reshape(count, width, count, width)
    selector = jnp.eye(count, dtype=upper.dtype)
    blocks = jnp.einsum("iajb,ij->iab", shaped, selector, precision=lax.Precision.HIGHEST)
    inverse = jnp.zeros_like(blocks)
    unit = jnp.eye(width, dtype=upper.dtype)
    for line in range(width - 1, -1, -1):
        known = jnp.einsum(
            "bj,bjc->bc", blocks[:, line, :], inverse, precision=lax.Precision.HIGHEST
        )
        value = (unit[line][None, :] - known) / blocks[:, line, line][:, None]
        inverse = inverse.at[:, line, :].set(value)
    span = width
    while count > 1:
        shaped = upper.reshape(count, span, count, span)
        pairs = count // 2
        lefts = jnp.arange(pairs) * 2
        pick = (
            (jnp.arange(count)[None, :, None] == lefts[:, None, None])
            & (jnp.arange(count)[None, None, :] == lefts[:, None, None] + 1)
        ).astype(upper.dtype)
        corner = jnp.einsum("iajb,pij->pab", shaped, pick, precision=lax.Precision.HIGHEST)
        first = inverse[0::2]
        second = inverse[1::2]
        top = -jnp.einsum(
            "pab,pbc->pac",
            jnp.einsum("pab,pbc->pac", first, corner, precision=lax.Precision.HIGHEST),
            second,
            precision=lax.Precision.HIGHEST,
        )
        upper_half = jnp.concatenate([first, top], axis=2)
        lower_half = jnp.concatenate([jnp.zeros_like(second), second], axis=2)
        inverse = jnp.concatenate([upper_half, lower_half], axis=1)
        count = pairs
        span = span * 2
    return inverse[0]


def tri_factor(gram):
    upper = jnp.triu(gram, 1) + jnp.diag(jnp.diag(gram)) * 0.5
    return tri_inverse(upper)


def tri_factor_doubling(gram):
    size = gram.shape[0]
    upper = jnp.triu(gram, 1) + jnp.diag(jnp.diag(gram)) * 0.5
    index = jnp.arange(size)
    same = index[:, None] == index[None, :]
    inverse = jnp.where(same, 1.0 / jnp.diag(upper)[None, :], 0.0)
    span = 1
    while span < size:
        group = index // (2 * span)
        side = (index // span) % 2
        corner = (group[:, None] == group[None, :]) & (side[:, None] == 0) & (side[None, :] == 1)
        inverse = inverse - dot_high(dot_high(inverse, jnp.where(corner, upper, 0.0)), inverse)
        span *= 2
    return inverse


def swap(value, distance, size):
    return lax.ppermute(value, "row", [(i, i ^ distance) for i in range(size)])


def spread(size):
    steps = []
    distance = 1
    while distance < size:
        steps.append(distance)
        distance *= 2
    return steps


def slot_order(me, size):
    steps = spread(size)
    order = []
    for slot in range(size):
        mask = 0
        for level, distance in enumerate(steps):
            if not (slot >> (len(steps) - 1 - level)) & 1:
                mask ^= distance
        order.append(mask)
    return jnp.array(order) ^ me


def col_sum(value):
    size = lax.axis_size("col")
    for distance in spread(size):
        value = value + lax.ppermute(
            value, "col", [(i, i ^ distance) for i in range(size)]
        )
    return value


def scatter_rows(value, size):
    for distance in spread(size):
        count = value.shape[0] // 2
        value = value[count:] + swap(value[:count], distance, size)
    return value


def shards(basis, panel_one, panel_two, gradient):
    size = lax.axis_size("row")
    k = panel_one.shape[1]
    span = panel_one.shape[0]
    lanes = gradient.shape[1] // size
    me = lax.axis_index("row")
    own = jnp.concatenate([panel_one, panel_two], axis=1)
    held = {0: own}
    beside = swap(own, 1, size)
    landed = own
    for distance in reversed(spread(size)):
        keys = [key for key in sorted(held) if distance > 1 or key]
        if distance == 1:
            held[1] = beside
        if keys:
            got = swap(jnp.stack([held[key] for key in keys]), distance, size)
            if distance > 1:
                landed = got
            for index, key in enumerate(keys):
                held[key ^ distance] = got[index]
    held = jnp.stack([held[key] for key in range(size)])

    order = slot_order(me, size)
    shuffled = jnp.take(gradient.reshape(-1, size, lanes), order, axis=1).reshape(gradient.shape)
    head = inner_mid(shuffled, basis)
    count = head.shape[0] // 2
    head = head[count:] + swap(head[:count], 1, size)

    gram_own = inner_rows(own, own)
    gram_chip = gram_own + swap(gram_own, 1, size)
    half = me % 2
    rows = gram_chip.shape[0] // 2
    mine = col_sum(lax.dynamic_slice_in_dim(gram_chip, half * rows, rows, axis=0))
    mine, head = lax.optimization_barrier((mine, head))
    for distance in spread(size)[1:]:
        mine = mine + swap(mine, distance, size)
    halves = jnp.stack([mine, swap(mine, 1, size)])
    gram = jnp.take(halves, jnp.array([0, 1]) ^ half, axis=0).reshape(2 * rows, -1)

    head, _ = lax.optimization_barrier((head, landed))
    for distance in spread(size)[1:]:
        count = head.shape[0] // 2
        head = head[count:] + swap(head[:count], distance, size)

    image = None
    for slot in range(size):
        cols = lax.dynamic_slice_in_dim(basis, (me ^ slot) * span, span, axis=1)
        part = dot_high(cols, held[slot])
        image = part if image is None else image + part
    image = jnp.concatenate([col_sum(image[:, :k]), col_sum(image[:, k:])], axis=1)

    gathered = jnp.take(held, jnp.arange(size) ^ me, axis=0).reshape(size * span, -1)
    factor_one = tri_factor_doubling(gram[:k, :k])
    factor_two = tri_factor_doubling(gram[k:, k:])
    first = dot_high(image[:, :k], factor_one)
    image_two = image[:, k:] - dot_high(first, gram[:k, k:])
    second = dot_high(image_two, factor_two)
    weight = jnp.concatenate([first, second], axis=1)
    new_basis = basis - outer_mid(weight, gathered)
    tail = scatter_rows(inner_rows(shuffled, weight), size)
    rotated = head - outer_mid(tail, gathered)
    return (new_basis, rotated)


def solution(mesh):
    return jax.shard_map(
        shards,
        mesh=mesh,
        in_specs=(
            P(("parts", "row"), "col"),
            P(("parts", "col", "row"), None),
            P(("parts", "col", "row"), None),
            P(("parts", "row"), None),
        ),
        out_specs=(P(("parts", "row"), "col"), P(("parts", "row"), "col")),
        check_vma=False,
    )
```

```python
import jax
import jax.numpy as jnp
from jax import lax
from jax.sharding import PartitionSpec as P


def dot_high(left, right):
    return jnp.dot(left, right, precision=lax.Precision.HIGHEST, preferred_element_type=jnp.float32)


def inner_rows(left, right):
    return jnp.einsum(
        "ra,rb->ab",
        left,
        right,
        precision=lax.Precision.HIGHEST,
        preferred_element_type=jnp.float32,
    )


def outer_cols(left, right):
    return jnp.einsum(
        "rk,ck->rc",
        left,
        right,
        precision=lax.Precision.HIGHEST,
        preferred_element_type=jnp.float32,
    )


def outer_mid(left, right):
    return jnp.einsum(
        "rk,ck->rc",
        left,
        right,
        precision=lax.Precision.HIGH,
        preferred_element_type=jnp.float32,
    )


def inner_mid(left, right):
    return jnp.einsum(
        "ra,rb->ab",
        left,
        right,
        precision=lax.Precision.HIGH,
        preferred_element_type=jnp.float32,
    )


def tri_inverse(upper):
    size = upper.shape[0]
    width = 8
    count = size // width
    shaped = upper.reshape(count, width, count, width)
    selector = jnp.eye(count, dtype=upper.dtype)
    blocks = jnp.einsum("iajb,ij->iab", shaped, selector, precision=lax.Precision.HIGHEST)
    inverse = jnp.zeros_like(blocks)
    unit = jnp.eye(width, dtype=upper.dtype)
    for line in range(width - 1, -1, -1):
        known = jnp.einsum(
            "bj,bjc->bc", blocks[:, line, :], inverse, precision=lax.Precision.HIGHEST
        )
        value = (unit[line][None, :] - known) / blocks[:, line, line][:, None]
        inverse = inverse.at[:, line, :].set(value)
    span = width
    while count > 1:
        shaped = upper.reshape(count, span, count, span)
        pairs = count // 2
        lefts = jnp.arange(pairs) * 2
        pick = (
            (jnp.arange(count)[None, :, None] == lefts[:, None, None])
            & (jnp.arange(count)[None, None, :] == lefts[:, None, None] + 1)
        ).astype(upper.dtype)
        corner = jnp.einsum("iajb,pij->pab", shaped, pick, precision=lax.Precision.HIGHEST)
        first = inverse[0::2]
        second = inverse[1::2]
        top = -jnp.einsum(
            "pab,pbc->pac",
            jnp.einsum("pab,pbc->pac", first, corner, precision=lax.Precision.HIGHEST),
            second,
            precision=lax.Precision.HIGHEST,
        )
        upper_half = jnp.concatenate([first, top], axis=2)
        lower_half = jnp.concatenate([jnp.zeros_like(second), second], axis=2)
        inverse = jnp.concatenate([upper_half, lower_half], axis=1)
        count = pairs
        span = span * 2
    return inverse[0]


def tri_factor(gram):
    upper = jnp.triu(gram, 1) + jnp.diag(jnp.diag(gram)) * 0.5
    return tri_inverse(upper)


def tri_factor_doubling(gram):
    size = gram.shape[0]
    upper = jnp.triu(gram, 1) + jnp.diag(jnp.diag(gram)) * 0.5
    index = jnp.arange(size)
    same = index[:, None] == index[None, :]
    inverse = jnp.where(same, 1.0 / jnp.diag(upper)[None, :], 0.0)
    span = 1
    while span < size:
        group = index // (2 * span)
        side = (index // span) % 2
        corner = (group[:, None] == group[None, :]) & (side[:, None] == 0) & (side[None, :] == 1)
        inverse = inverse - dot_high(dot_high(inverse, jnp.where(corner, upper, 0.0)), inverse)
        span *= 2
    return inverse


def swap(value, distance, size):
    return lax.ppermute(value, "row", [(i, i ^ distance) for i in range(size)])


def spread(size):
    steps = []
    distance = 1
    while distance < size:
        steps.append(distance)
        distance *= 2
    return steps


def slot_order(me, size):
    steps = spread(size)
    order = []
    for slot in range(size):
        mask = 0
        for level, distance in enumerate(steps):
            if not (slot >> (len(steps) - 1 - level)) & 1:
                mask ^= distance
        order.append(mask)
    return jnp.array(order) ^ me


def col_sum(value):
    size = lax.axis_size("col")
    for distance in spread(size):
        value = value + lax.ppermute(
            value, "col", [(i, i ^ distance) for i in range(size)]
        )
    return value


def scatter_rows(value, size):
    for distance in spread(size):
        count = value.shape[0] // 2
        value = value[count:] + swap(value[:count], distance, size)
    return value


def shards(basis, panel_one, panel_two, gradient):
    size = lax.axis_size("row")
    k = panel_one.shape[1]
    span = panel_one.shape[0]
    lanes = gradient.shape[1] // size
    me = lax.axis_index("row")
    own = jnp.concatenate([panel_one, panel_two], axis=1)
    held = {0: own}
    beside = swap(own, 1, size)
    landed = own
    for distance in reversed(spread(size)):
        keys = [key for key in sorted(held) if distance > 1 or key]
        if distance == 1:
            held[1] = beside
        if keys:
            got = swap(jnp.stack([held[key] for key in keys]), distance, size)
            if distance > 1:
                landed = got
            for index, key in enumerate(keys):
                held[key ^ distance] = got[index]
    held = jnp.stack([held[key] for key in range(size)])

    order = slot_order(me, size)
    shuffled = jnp.take(gradient.reshape(-1, size, lanes), order, axis=1).reshape(gradient.shape)
    head = inner_mid(shuffled, basis)
    count = head.shape[0] // 2
    head = head[count:] + swap(head[:count], 1, size)

    gram_own = inner_rows(own, own)
    gram_chip = gram_own + swap(gram_own, 1, size)
    half = me % 2
    rows = gram_chip.shape[0] // 2
    mine = col_sum(lax.dynamic_slice_in_dim(gram_chip, half * rows, rows, axis=0))
    mine, head = lax.optimization_barrier((mine, head))
    for distance in spread(size)[1:]:
        mine = mine + swap(mine, distance, size)
    halves = jnp.stack([mine, swap(mine, 1, size)])
    gram = jnp.take(halves, jnp.array([0, 1]) ^ half, axis=0).reshape(2 * rows, -1)

    head, _ = lax.optimization_barrier((head, landed))
    for distance in spread(size)[1:]:
        count = head.shape[0] // 2
        head = head[count:] + swap(head[:count], distance, size)

    image = None
    for slot in range(size):
        cols = lax.dynamic_slice_in_dim(basis, (me ^ slot) * span, span, axis=1)
        part = dot_high(cols, held[slot])
        image = part if image is None else image + part
    quarter = k // 2
    image = jnp.concatenate(
        [col_sum(image[:, at : at + quarter]) for at in range(0, 2 * k, quarter)], axis=1
    )

    gathered = jnp.take(held, jnp.arange(size) ^ me, axis=0).reshape(size * span, -1)
    factor_one = tri_factor_doubling(gram[:k, :k])
    factor_two = tri_factor_doubling(gram[k:, k:])
    first = dot_high(image[:, :k], factor_one)
    image_two = image[:, k:] - dot_high(first, gram[:k, k:])
    second = dot_high(image_two, factor_two)
    weight = jnp.concatenate([first, second], axis=1)
    new_basis = basis - outer_mid(weight, gathered)
    tail = scatter_rows(inner_rows(shuffled, weight), size)
    rotated = head - outer_mid(tail, gathered)
    return (new_basis, rotated)


def solution(mesh):
    return jax.shard_map(
        shards,
        mesh=mesh,
        in_specs=(
            P(("parts", "row"), "col"),
            P(("parts", "col", "row"), None),
            P(("parts", "col", "row"), None),
            P(("parts", "row"), None),
        ),
        out_specs=(P(("parts", "row"), "col"), P(("parts", "row"), "col")),
        check_vma=False,
    )
```

```python
import jax
import jax.numpy as jnp
from jax import lax
from jax.sharding import PartitionSpec as P


def dot_high(left, right):
    return jnp.dot(left, right, precision=lax.Precision.HIGHEST, preferred_element_type=jnp.float32)


def inner_rows(left, right):
    return jnp.einsum(
        "ra,rb->ab",
        left,
        right,
        precision=lax.Precision.HIGHEST,
        preferred_element_type=jnp.float32,
    )


def outer_cols(left, right):
    return jnp.einsum(
        "rk,ck->rc",
        left,
        right,
        precision=lax.Precision.HIGHEST,
        preferred_element_type=jnp.float32,
    )


def outer_mid(left, right):
    return jnp.einsum(
        "rk,ck->rc",
        left,
        right,
        precision=lax.Precision.HIGH,
        preferred_element_type=jnp.float32,
    )


def inner_mid(left, right):
    return jnp.einsum(
        "ra,rb->ab",
        left,
        right,
        precision=lax.Precision.HIGH,
        preferred_element_type=jnp.float32,
    )


def tri_inverse(upper):
    size = upper.shape[0]
    width = 8
    count = size // width
    shaped = upper.reshape(count, width, count, width)
    selector = jnp.eye(count, dtype=upper.dtype)
    blocks = jnp.einsum("iajb,ij->iab", shaped, selector, precision=lax.Precision.HIGHEST)
    inverse = jnp.zeros_like(blocks)
    unit = jnp.eye(width, dtype=upper.dtype)
    for line in range(width - 1, -1, -1):
        known = jnp.einsum(
            "bj,bjc->bc", blocks[:, line, :], inverse, precision=lax.Precision.HIGHEST
        )
        value = (unit[line][None, :] - known) / blocks[:, line, line][:, None]
        inverse = inverse.at[:, line, :].set(value)
    span = width
    while count > 1:
        shaped = upper.reshape(count, span, count, span)
        pairs = count // 2
        lefts = jnp.arange(pairs) * 2
        pick = (
            (jnp.arange(count)[None, :, None] == lefts[:, None, None])
            & (jnp.arange(count)[None, None, :] == lefts[:, None, None] + 1)
        ).astype(upper.dtype)
        corner = jnp.einsum("iajb,pij->pab", shaped, pick, precision=lax.Precision.HIGHEST)
        first = inverse[0::2]
        second = inverse[1::2]
        top = -jnp.einsum(
            "pab,pbc->pac",
            jnp.einsum("pab,pbc->pac", first, corner, precision=lax.Precision.HIGHEST),
            second,
            precision=lax.Precision.HIGHEST,
        )
        upper_half = jnp.concatenate([first, top], axis=2)
        lower_half = jnp.concatenate([jnp.zeros_like(second), second], axis=2)
        inverse = jnp.concatenate([upper_half, lower_half], axis=1)
        count = pairs
        span = span * 2
    return inverse[0]


def tri_factor(gram):
    upper = jnp.triu(gram, 1) + jnp.diag(jnp.diag(gram)) * 0.5
    return tri_inverse(upper)


def tri_factor_doubling(gram):
    size = gram.shape[0]
    upper = jnp.triu(gram, 1) + jnp.diag(jnp.diag(gram)) * 0.5
    index = jnp.arange(size)
    same = index[:, None] == index[None, :]
    inverse = jnp.where(same, 1.0 / jnp.diag(upper)[None, :], 0.0)
    span = 1
    while span < size:
        group = index // (2 * span)
        side = (index // span) % 2
        corner = (group[:, None] == group[None, :]) & (side[:, None] == 0) & (side[None, :] == 1)
        inverse = inverse - dot_high(dot_high(inverse, jnp.where(corner, upper, 0.0)), inverse)
        span *= 2
    return inverse


def swap(value, distance, size):
    return lax.ppermute(value, "row", [(i, i ^ distance) for i in range(size)])


def spread(size):
    steps = []
    distance = 1
    while distance < size:
        steps.append(distance)
        distance *= 2
    return steps


def slot_order(me, size):
    steps = spread(size)
    order = []
    for slot in range(size):
        mask = 0
        for level, distance in enumerate(steps):
            if not (slot >> (len(steps) - 1 - level)) & 1:
                mask ^= distance
        order.append(mask)
    return jnp.array(order) ^ me


def col_sum(value):
    size = lax.axis_size("col")
    for distance in spread(size):
        value = value + lax.ppermute(
            value, "col", [(i, i ^ distance) for i in range(size)]
        )
    return value


def scatter_rows(value, size):
    for distance in spread(size):
        count = value.shape[0] // 2
        value = value[count:] + swap(value[:count], distance, size)
    return value


def shards(basis, panel_one, panel_two, gradient):
    size = lax.axis_size("row")
    k = panel_one.shape[1]
    span = panel_one.shape[0]
    lanes = gradient.shape[1] // size
    me = lax.axis_index("row")
    own = jnp.concatenate([panel_one, panel_two], axis=1)
    held = {0: own}
    beside = swap(own, 1, size)
    landed = own
    for distance in reversed(spread(size)):
        keys = [key for key in sorted(held) if distance > 1 or key]
        if distance == 1:
            held[1] = beside
        if keys:
            got = swap(jnp.stack([held[key] for key in keys]), distance, size)
            if distance > 1:
                landed = got
            for index, key in enumerate(keys):
                held[key ^ distance] = got[index]
    held = jnp.stack([held[key] for key in range(size)])

    order = slot_order(me, size)
    shuffled = jnp.take(gradient.reshape(-1, size, lanes), order, axis=1).reshape(gradient.shape)
    head = inner_mid(shuffled, basis)
    count = head.shape[0] // 2
    head = head[count:] + swap(head[:count], 1, size)

    gram_own = inner_rows(own, own)
    gram_chip = gram_own + swap(gram_own, 1, size)
    half = me % 2
    rows = gram_chip.shape[0] // 2
    mine = lax.dynamic_slice_in_dim(gram_chip, half * rows, rows, axis=0)
    mine = jnp.concatenate([col_sum(mine[:, :k]), col_sum(mine[:, k:])], axis=1)
    mine, head = lax.optimization_barrier((mine, head))
    for distance in spread(size)[1:]:
        mine = mine + swap(mine, distance, size)
    halves = jnp.stack([mine, swap(mine, 1, size)])
    gram = jnp.take(halves, jnp.array([0, 1]) ^ half, axis=0).reshape(2 * rows, -1)

    head, _ = lax.optimization_barrier((head, landed))
    for distance in spread(size)[1:]:
        count = head.shape[0] // 2
        head = head[count:] + swap(head[:count], distance, size)

    image = None
    for slot in range(size):
        cols = lax.dynamic_slice_in_dim(basis, (me ^ slot) * span, span, axis=1)
        part = dot_high(cols, held[slot])
        image = part if image is None else image + part
    image = jnp.concatenate([col_sum(image[:, :k]), col_sum(image[:, k:])], axis=1)

    gathered = jnp.take(held, jnp.arange(size) ^ me, axis=0).reshape(size * span, -1)
    factor_one = tri_factor_doubling(gram[:k, :k])
    factor_two = tri_factor_doubling(gram[k:, k:])
    first = dot_high(image[:, :k], factor_one)
    image_two = image[:, k:] - dot_high(first, gram[:k, k:])
    second = dot_high(image_two, factor_two)
    weight = jnp.concatenate([first, second], axis=1)
    new_basis = basis - outer_mid(weight, gathered)
    tail = scatter_rows(inner_rows(shuffled, weight), size)
    rotated = head - outer_mid(tail, gathered)
    return (new_basis, rotated)


def solution(mesh):
    return jax.shard_map(
        shards,
        mesh=mesh,
        in_specs=(
            P(("parts", "row"), "col"),
            P(("parts", "col", "row"), None),
            P(("parts", "col", "row"), None),
            P(("parts", "row"), None),
        ),
        out_specs=(P(("parts", "row"), "col"), P(("parts", "row"), "col")),
        check_vma=False,
    )
```
